768 devices in a mesh: node: 12 (over z), section: 64 (over y, x, core).
Axes of the slice: x: 4, y: 8, z: 12, core: 2. Of those that a mesh axis runs over, the one named last changes fastest.
Arguments:
- tokens: bfloat16 [64, 3072, 512], P('section', 'node'), may hold values from -6 to 6
- cotangent: bfloat16 [64, 3072, 512], P('section', 'node'), may hold values from -6 to 6
- w_qkv: bfloat16 [512, 1536], replicated
- w_out: bfloat16 [512, 512], replicated, may hold values from -2.09375 to 2.09375
- norm_gain: float32 [512], replicated, may hold values from 0.1 to 1.9
- tile_lists: int32 [24, 5], replicated, may hold values from 0 to 23, as said below
- tile_counts: int32 [24], replicated, may hold values from 3 to 5, as said below
Outputs:
- mixed_tokens: bfloat16 [64, 3072, 512], P('section', 'node')
- grad_tokens: bfloat16 [64, 3072, 512], P('section', 'node')
- grad_w_qkv: float32 [512, 1536], P('section', 'node')
- grad_w_out: float32 [512, 512], P('section')
- grad_gain: float32 [512], P('section')
The draws below stay inside these ranges and needn't reach their ends.
Inputs may be any that keep to these rules, and one draw needn't show every extreme that they name: `tile_lists`: tiles are numbered in order, 2 to a block, the first and last blocks counting as adjacent; entry 0 of row t is t itself, entry 1 lies in the block just before t's block, entry 2 in the block just after it, the other entries in one of these three blocks; the entries of a row are distinct. `tile_counts`: some tile has 5.
All inputs are finite; a program needn't handle non-finite values.
Results may differ from the reference program's by a relative error of at most 0.017.
Values may be sent and summed in bfloat16 or wider, within the bound.
No kernel may reach another device: no remote copies, remote signals or barrier semaphores. Data moves between devices by JAX's collectives and lax.ppermute only.
A program may use at most 64 MiB of HBM per device.

```python
import jax
import jax.numpy as jnp
from jax import lax

D = 512
HEADS = 4
TILE = 128
TPD = 2
NB = 5
MEMBERS = 64
NTILES = 24
NODES = 3072
N_NODE = 12


def draw_w_qkv(key, part):
    key_one, key_two, key_three = jax.random.split(jax.random.fold_in(key, 17), 3)
    fan_scale = D ** (-0.5)
    value_part = jax.random.normal(key_three, (D, D), jnp.float32) * fan_scale
    query_part = jax.random.normal(key_one, (D, D), jnp.float32) * fan_scale
    key_part = jax.random.normal(key_two, (D, D), jnp.float32) * fan_scale
    return jnp.concatenate([query_part, key_part, value_part], axis=1).astype(jnp.bfloat16)


def draw_tile_lists(key, part):
    span_tiles = 3 * TPD
    own_tile = jnp.arange(NTILES, dtype=jnp.int32)
    block_index = own_tile // TPD
    inside = own_tile - block_index * TPD
    window_slots = jnp.arange(span_tiles, dtype=jnp.int32)
    ranking = jax.random.randint(jax.random.fold_in(key, 23), (NTILES, span_tiles), 0, 1 << 20) * 64 + window_slots[None, :]
    before_slot = jax.random.randint(jax.random.fold_in(key, 31), (NTILES,), 0, TPD)
    after_slot = 2 * TPD + jax.random.randint(jax.random.fold_in(key, 37), (NTILES,), 0, TPD)
    self_slot = TPD + inside
    ranking = jnp.where(window_slots[None, :] == after_slot[:, None], -1, ranking)
    ranking = jnp.where(window_slots[None, :] == before_slot[:, None], -2, ranking)
    ranking = jnp.where(window_slots[None, :] == self_slot[:, None], -3, ranking)
    chosen = jnp.argsort(ranking, axis=1)[:, :NB].astype(jnp.int32)
    tile_ids = jnp.mod((block_index[:, None] - 1) * TPD + chosen, NTILES)
    return tile_ids.astype(jnp.int32)


def draw_tile_counts(key, part):
    key_one, key_two = jax.random.split(jax.random.fold_in(key, 29))
    counts = jax.random.randint(key_one, (NTILES,), 3, NB + 1)
    fullest = jax.random.randint(key_two, (), 0, NTILES)
    return jnp.where(jnp.arange(NTILES, dtype=jnp.int32) == fullest, NB, counts).astype(jnp.int32)


def block_scale(own_key, shape, shards, smallest, top_value):
    gain, own = 1.0, jax.random.fold_in(own_key, 6)
    for dim, shards_of in shards:
        steps = jnp.exp(jax.random.uniform(jax.random.fold_in(own, dim), (shards_of,), jnp.float32, smallest / len(shards), top_value / len(shards)))
        gain = gain * jnp.repeat(steps, shape[dim] // shards_of).reshape([-1 if axis == dim else 1 for axis in range(len(shape))])
    return gain


def bell_draw(key, shape, width, most, pieces=(), kind=jnp.bfloat16):
    gain = block_scale(key, shape, pieces, -0.22, 0.18) if pieces else 1.0
    drawn = jax.random.normal(key, shape, jnp.float32) * width * gain
    return jnp.minimum(jnp.maximum(drawn, -most), most).astype(kind)


def setup_inputs(seed: int = 0) -> dict:
    arg_keys = jax.random.split(jax.random.key(seed), 8)
    return {
        "tokens": bell_draw(arg_keys[0], (MEMBERS, NODES, D), 1.0, 6.0, ((0, 64), (1, 12))),
        "cotangent": bell_draw(arg_keys[1], (MEMBERS, NODES, D), 1.0, 6.0, ((0, 64), (1, 12))),
        "w_qkv": draw_w_qkv(jax.random.fold_in(arg_keys[7], 71), 0),
        "w_out": bell_draw(arg_keys[3], (D, D), 0.35, 2.09375),
        "norm_gain": jnp.clip(1.0 + 0.18 * jax.random.normal(arg_keys[4], (D,), jnp.float32), 0.1, 1.9),
        "tile_lists": draw_tile_lists(jax.random.fold_in(arg_keys[7], 71), 0),
        "tile_counts": draw_tile_counts(jax.random.fold_in(arg_keys[7], 71), 0),
    }


EPS = 1e-06
MASKED = -1000000000.0

def tile_mask(own_lists, own_counts, first_tile, tile_total):
    tile_count = own_lists.shape[0]
    span_tiles = 3 * tile_count
    places = jnp.mod(own_lists - first_tile, tile_total)
    live_entries = jnp.arange(own_lists.shape[1], dtype=jnp.int32)[None, :] < own_counts[:, None]
    window_slots = jnp.arange(span_tiles, dtype=jnp.int32)
    matches = jnp.logical_and(places[:, :, None] == window_slots[None, None, :], live_entries[:, :, None])
    return jnp.any(matches, axis=1)

def attend(queries, window_keys, window_values, allowed):
    row_count, model_width = queries.shape
    tile_count, span_tiles = allowed.shape
    head_dim = model_width // HEADS
    score_scale = head_dim ** (-0.5)
    query_heads = queries.astype(jnp.float32).reshape(tile_count, TILE, HEADS, head_dim)
    key_heads = window_keys.astype(jnp.float32).reshape(span_tiles, TILE, HEADS, head_dim)
    value_heads = window_values.astype(jnp.float32).reshape(span_tiles, TILE, HEADS, head_dim)
    scores = jnp.einsum('atnd,bsnd->natbs', query_heads, key_heads) * score_scale
    scores = jnp.where(allowed[None, :, None, :, None], scores, MASKED)
    row_peak = lax.optimization_barrier(jnp.max(scores, axis=(3, 4), keepdims=True))
    expanded = jnp.exp(scores - row_peak)
    probabilities = expanded / lax.optimization_barrier(jnp.sum(expanded, axis=(3, 4), keepdims=True))
    rounded = probabilities.astype(jnp.bfloat16)
    attended = jnp.einsum('natbs,bsnd->atnd', rounded.astype(jnp.float32), value_heads)
    return (attended.reshape(row_count, model_width).astype(jnp.bfloat16), probabilities, rounded)

def attend_back(grad_attended, queries, window_keys, window_values, probabilities, rounded):
    row_count, model_width = queries.shape
    tile_count = probabilities.shape[1]
    span_tiles = probabilities.shape[3]
    head_dim = model_width // HEADS
    score_scale = head_dim ** (-0.5)
    query_heads = queries.astype(jnp.float32).reshape(tile_count, TILE, HEADS, head_dim)
    key_heads = window_keys.astype(jnp.float32).reshape(span_tiles, TILE, HEADS, head_dim)
    value_heads = window_values.astype(jnp.float32).reshape(span_tiles, TILE, HEADS, head_dim)
    grad_heads = grad_attended.astype(jnp.float32).reshape(tile_count, TILE, HEADS, head_dim)
    grad_probs = jnp.einsum('atnd,bsnd->natbs', grad_heads, value_heads)
    centre = lax.optimization_barrier(jnp.sum(grad_probs * probabilities, axis=(3, 4), keepdims=True))
    grad_scores = (probabilities * (grad_probs - centre) * score_scale).astype(jnp.bfloat16)
    scores_wide = grad_scores.astype(jnp.float32)
    grad_queries = jnp.einsum('natbs,bsnd->atnd', scores_wide, key_heads).reshape(row_count, model_width)
    grad_keys = jnp.einsum('natbs,atnd->bsnd', scores_wide, query_heads).reshape(span_tiles * TILE, model_width)
    grad_values = jnp.einsum('natbs,atnd->bsnd', rounded.astype(jnp.float32), grad_heads).reshape(span_tiles * TILE, model_width)
    return (grad_queries, jnp.concatenate([grad_keys, grad_values], axis=1))

def member_pass(tokens_one, grad_one, w_qkv, w_out, norm_gain, masks):
    row_count = TPD * TILE
    model_width = tokens_one.shape[1]
    widened = tokens_one.astype(jnp.float32).reshape(N_NODE, row_count, model_width)
    inverse_rms = lax.rsqrt(lax.optimization_barrier(jnp.mean(widened * widened, axis=-1, keepdims=True)) + EPS)
    unit_rows = widened * inverse_rms
    normed = (unit_rows * norm_gain).astype(jnp.bfloat16)
    flat_normed = normed.reshape(-1, model_width)
    projected = jnp.dot(flat_normed, w_qkv, preferred_element_type=jnp.float32).astype(jnp.bfloat16)
    projected = projected.reshape(N_NODE, row_count, 3 * model_width)
    queries = projected[:, :, :model_width]
    keyvals = projected[:, :, model_width:]
    window = jnp.concatenate([jnp.roll(keyvals, 1, axis=0), keyvals, jnp.roll(keyvals, -1, axis=0)], axis=1)
    window_keys = window[:, :, :model_width]
    window_values = window[:, :, model_width:]
    attended, probabilities, rounded = jax.vmap(attend)(queries, window_keys, window_values, masks)
    flat_attended = attended.reshape(-1, model_width)
    grad_flat = grad_one.reshape(-1, model_width)
    outputs = (widened.reshape(-1, model_width) + jnp.dot(flat_attended, w_out, preferred_element_type=jnp.float32)).astype(jnp.bfloat16)
    term_out = jnp.dot(flat_attended.T, grad_flat, preferred_element_type=jnp.float32)
    grad_attended = jnp.dot(grad_flat, w_out.T, preferred_element_type=jnp.float32).astype(jnp.bfloat16)
    grad_attended = grad_attended.reshape(N_NODE, row_count, model_width)
    grad_queries, grad_window = jax.vmap(attend_back)(grad_attended, queries, window_keys, window_values, probabilities, rounded)
    grad_keyvals = grad_window[:, row_count:2 * row_count]
    grad_keyvals = grad_keyvals + jnp.roll(grad_window[:, :row_count], -1, axis=0)
    grad_keyvals = grad_keyvals + jnp.roll(grad_window[:, 2 * row_count:], 1, axis=0)
    grad_projected = jnp.concatenate([grad_queries, grad_keyvals], axis=-1).astype(jnp.bfloat16)
    grad_projected = grad_projected.reshape(-1, 3 * model_width)
    term_qkv = jnp.dot(flat_normed.T, grad_projected, preferred_element_type=jnp.float32)
    grad_normed = jnp.dot(grad_projected, w_qkv.T, preferred_element_type=jnp.float32)
    flat_unit = unit_rows.reshape(-1, model_width)
    term_gain = lax.optimization_barrier(jnp.sum(grad_normed * flat_unit, axis=0))
    grad_unit = grad_normed * norm_gain
    inner_mean = lax.optimization_barrier(jnp.mean(grad_unit * flat_unit, axis=-1, keepdims=True))
    grad_tokens = grad_flat.astype(jnp.float32) + inverse_rms.reshape(-1, 1) * (grad_unit - flat_unit * inner_mean)
    return (outputs, grad_tokens.astype(jnp.bfloat16), term_qkv, term_out, term_gain)

def reference(tokens, cotangent, w_qkv, w_out, norm_gain, tile_lists, tile_counts):
    model_width = tokens.shape[2]
    node_lists = tile_lists.reshape(N_NODE, TPD, NB)
    node_counts = tile_counts.reshape(N_NODE, TPD)
    first_tiles = (jnp.arange(N_NODE, dtype=jnp.int32) - 1) * TPD
    masks = jax.vmap(tile_mask, in_axes=(0, 0, 0, None))(node_lists, node_counts, first_tiles, NTILES)

    def member_step(totals, slices):
        outputs, grad_tokens, term_qkv, term_out, term_gain = member_pass(slices[0], slices[1], w_qkv, w_out, norm_gain, masks)
        return ((totals[0] + term_qkv, totals[1] + term_out, totals[2] + term_gain), (outputs, grad_tokens))
    start_sums = (jnp.zeros((model_width, 3 * model_width), jnp.float32), jnp.zeros((model_width, model_width), jnp.float32), jnp.zeros((model_width,), jnp.float32))
    sums, stacked = lax.scan(member_step, start_sums, (tokens, cotangent))
    mixed_tokens = stacked[0].reshape(tokens.shape)
    grad_tokens = stacked[1].reshape(tokens.shape)
    return (mixed_tokens, grad_tokens, sums[0], sums[1], sums[2])
```

```python
import jax
import jax.numpy as jnp
from jax import lax
from jax.sharding import Mesh, PartitionSpec as P

HEADS = 4
TILE = 128


EPS = 1e-06
MASKED = -1000000000.0


def extended(block, sides, width):
    for axis, dim in sides:
        count = lax.axis_size(axis)
        forward = [(i, i + 1) for i in range(count - 1)]
        forward.append((count - 1, 0))
        backward = [(target, source) for source, target in forward]
        low = lax.ppermute(
            lax.slice_in_dim(block, block.shape[dim] - width, None, axis=dim), axis, forward
        )
        high = lax.ppermute(lax.slice_in_dim(block, 0, width, axis=dim), axis, backward)
        block = jnp.concatenate([low, block, high], axis=dim)
    return block


def passed_along(block, axis, distance):
    devices = range(lax.axis_size(axis))
    route = [((i - distance) % len(devices), i) for i in devices]
    return lax.ppermute(block, axis, route)


def tile_mask(own_lists, own_counts, first_tile, tile_total):
    tile_count = own_lists.shape[0]
    span_tiles = 3 * tile_count
    places = jnp.mod(own_lists - first_tile, tile_total)
    live_entries = jnp.arange(own_lists.shape[1], dtype=jnp.int32)[None, :] < own_counts[:, None]
    window_slots = jnp.arange(span_tiles, dtype=jnp.int32)
    matches = jnp.logical_and(
        places[:, :, None] == window_slots[None, None, :], live_entries[:, :, None]
    )
    return jnp.any(matches, axis=1)


def attend(queries, window_keys, window_values, allowed):
    row_count, model_width = queries.shape
    tile_count, span_tiles = allowed.shape
    head_dim = model_width // HEADS
    score_scale = head_dim ** (-0.5)
    query_heads = queries.reshape(tile_count, TILE, HEADS, head_dim)
    key_heads = window_keys.reshape(span_tiles, TILE, HEADS, head_dim)
    value_heads = window_values.reshape(span_tiles, TILE, HEADS, head_dim)
    scores = (
        jnp.einsum("atnd,bsnd->natbs", query_heads, key_heads, preferred_element_type=jnp.float32)
        * score_scale
    )
    scores = jnp.where(allowed[None, :, None, :, None], scores, MASKED)
    row_peak = jnp.max(scores, axis=(3, 4), keepdims=True)
    expanded = jnp.exp(scores - row_peak)
    probabilities = expanded / jnp.sum(expanded, axis=(3, 4), keepdims=True)
    rounded = probabilities.astype(jnp.bfloat16)
    attended = jnp.einsum(
        "natbs,bsnd->atnd", rounded, value_heads, preferred_element_type=jnp.float32
    )
    return (attended.reshape(row_count, model_width).astype(jnp.bfloat16), probabilities, rounded)


def attend_back(grad_attended, queries, window_keys, window_values, probabilities, rounded):
    row_count, model_width = queries.shape
    tile_count = probabilities.shape[1]
    span_tiles = probabilities.shape[3]
    head_dim = model_width // HEADS
    score_scale = head_dim ** (-0.5)
    query_heads = queries.reshape(tile_count, TILE, HEADS, head_dim)
    key_heads = window_keys.reshape(span_tiles, TILE, HEADS, head_dim)
    value_heads = window_values.reshape(span_tiles, TILE, HEADS, head_dim)
    grad_heads = grad_attended.reshape(tile_count, TILE, HEADS, head_dim)
    grad_probs = jnp.einsum(
        "atnd,bsnd->natbs", grad_heads, value_heads, preferred_element_type=jnp.float32
    )
    centre = jnp.sum(grad_probs * probabilities, axis=(3, 4), keepdims=True)
    grad_scores = (probabilities * (grad_probs - centre) * score_scale).astype(jnp.bfloat16)
    grad_queries = jnp.einsum(
        "natbs,bsnd->atnd", grad_scores, key_heads, preferred_element_type=jnp.float32
    ).reshape(row_count, model_width)
    grad_keys = jnp.einsum(
        "natbs,atnd->bsnd", grad_scores, query_heads, preferred_element_type=jnp.float32
    ).reshape(span_tiles * TILE, model_width)
    grad_values = jnp.einsum(
        "natbs,atnd->bsnd", rounded, grad_heads, preferred_element_type=jnp.float32
    ).reshape(span_tiles * TILE, model_width)
    return (grad_queries, jnp.concatenate([grad_keys, grad_values], axis=1))


def on_device(tokens, cotangent, w_qkv, w_out, norm_gain, tile_lists, tile_counts):
    own_tokens = tokens[0]
    own_grads = cotangent[0]
    row_count, model_width = own_tokens.shape
    tile_count = row_count // TILE
    tile_total = tile_lists.shape[0]
    device = lax.axis_index("node")
    own_lists = lax.dynamic_slice_in_dim(tile_lists, device * tile_count, tile_count, 0)
    own_counts = lax.dynamic_slice_in_dim(tile_counts, device * tile_count, tile_count, 0)
    allowed = tile_mask(own_lists, own_counts, (device - 1) * tile_count, tile_total)
    widened = own_tokens.astype(jnp.float32)
    inverse_rms = lax.rsqrt(jnp.mean(widened * widened, axis=-1, keepdims=True) + EPS)
    unit_rows = widened * inverse_rms
    normed = (unit_rows * norm_gain).astype(jnp.bfloat16)
    projected = jnp.dot(normed, w_qkv, preferred_element_type=jnp.float32).astype(jnp.bfloat16)
    queries = projected[:, :model_width]
    window = extended(projected[:, model_width:], (("node", 0),), row_count)
    window_keys = window[:, :model_width]
    window_values = window[:, model_width:]
    attended, probabilities, rounded = attend(queries, window_keys, window_values, allowed)
    outputs = (widened + jnp.dot(attended, w_out, preferred_element_type=jnp.float32)).astype(
        jnp.bfloat16
    )
    contract_rows = (((0,), (0,)), ((), ()))
    contract_cols = (((1,), (1,)), ((), ()))
    term_out = lax.dot_general(
        attended, own_grads, contract_rows, preferred_element_type=jnp.float32
    )
    grad_attended = lax.dot_general(
        own_grads, w_out, contract_cols, preferred_element_type=jnp.float32
    ).astype(jnp.bfloat16)
    grad_queries, grad_window = attend_back(
        grad_attended, queries, window_keys, window_values, probabilities, rounded
    )
    grad_keyvals = grad_window[row_count : 2 * row_count]
    for offset, side_index in ((-1, 0), (1, 2)):
        side_part = grad_window[side_index * row_count : (side_index + 1) * row_count]
        grad_keyvals = grad_keyvals + passed_along(
            side_part.astype(jnp.bfloat16), "node", offset
        ).astype(side_part.dtype)
    grad_projected = jnp.concatenate([grad_queries, grad_keyvals], axis=1).astype(jnp.bfloat16)
    term_qkv = lax.dot_general(
        normed, grad_projected, contract_rows, preferred_element_type=jnp.float32
    )
    grad_normed = lax.dot_general(
        grad_projected, w_qkv, contract_cols, preferred_element_type=jnp.float32
    )
    term_gain = jnp.sum(grad_normed * unit_rows, axis=0)
    grad_unit = grad_normed * norm_gain
    inner_mean = jnp.mean(grad_unit * unit_rows, axis=-1, keepdims=True)
    grad_tokens = (
        own_grads.astype(jnp.float32) + inverse_rms * (grad_unit - unit_rows * inner_mean)
    ).astype(jnp.bfloat16)
    return (outputs[None], grad_tokens[None]) + reduce_terms(term_qkv, term_out, term_gain)


def section_order(rows):
    y_size, x_size, core_size = lax.axis_size("y"), lax.axis_size("x"), lax.axis_size("core")
    shape = rows.shape
    split = rows.reshape((y_size, x_size, core_size, -1) + shape[1:])
    return jnp.moveaxis(split, (2, 1, 0), (0, 1, 2)).reshape(shape)


def reduce_terms(term_qkv, term_out, term_gain):
    parts = (section_order(term_qkv), section_order(term_out), section_order(term_gain))
    for axis in ("core", "x", "y"):
        parts = tuple(lax.psum_scatter(p, axis, scatter_dimension=0, tiled=True) for p in parts)
    part_qkv, part_out, part_gain = parts
    part_qkv = lax.psum_scatter(part_qkv, "node", scatter_dimension=1, tiled=True)
    part_out, part_gain = lax.psum((part_out, part_gain), "node")
    return (part_qkv, part_out, part_gain)


def solution(mesh):
    node_size, section_size = mesh.devices.shape
    core_size = 2
    x_size = 4
    y_size = section_size // (core_size * x_size)
    fine = Mesh(mesh.devices.reshape(node_size, y_size, x_size, core_size), ("node", "y", "x", "core"))
    section = ("y", "x", "core")
    return jax.shard_map(
        on_device,
        mesh=fine,
        in_specs=(P(section, "node", None), P(section, "node", None), P(), P(), P(), P(), P()),
        out_specs=(
            P(section, "node", None),
            P(section, "node", None),
            P(section, "node"),
            P(section, None),
            P(section),
        ),
        check_vma=False,
    )
```

```python
import jax
import jax.numpy as jnp
from jax import lax
from jax.sharding import Mesh, PartitionSpec as P

HEADS = 4
TILE = 128


EPS = 1e-06
MASKED = -1000000000.0


def extended(block, sides, width):
    for axis, dim in sides:
        count = lax.axis_size(axis)
        forward = [(i, i + 1) for i in range(count - 1)]
        forward.append((count - 1, 0))
        backward = [(target, source) for source, target in forward]
        low = lax.ppermute(
            lax.slice_in_dim(block, block.shape[dim] - width, None, axis=dim), axis, forward
        )
        high = lax.ppermute(lax.slice_in_dim(block, 0, width, axis=dim), axis, backward)
        block = jnp.concatenate([low, block, high], axis=dim)
    return block


def passed_along(block, axis, distance):
    devices = range(lax.axis_size(axis))
    route = [((i - distance) % len(devices), i) for i in devices]
    return lax.ppermute(block, axis, route)


def tile_mask(own_lists, own_counts, first_tile, tile_total):
    tile_count = own_lists.shape[0]
    span_tiles = 3 * tile_count
    places = jnp.mod(own_lists - first_tile, tile_total)
    live_entries = jnp.arange(own_lists.shape[1], dtype=jnp.int32)[None, :] < own_counts[:, None]
    window_slots = jnp.arange(span_tiles, dtype=jnp.int32)
    matches = jnp.logical_and(
        places[:, :, None] == window_slots[None, None, :], live_entries[:, :, None]
    )
    return jnp.any(matches, axis=1)


def attend(queries, window_keys, window_values, allowed):
    row_count, model_width = queries.shape
    tile_count, span_tiles = allowed.shape
    head_dim = model_width // HEADS
    score_scale = head_dim ** (-0.5)
    query_heads = queries.reshape(tile_count, TILE, HEADS, head_dim)
    key_heads = window_keys.reshape(span_tiles, TILE, HEADS, head_dim)
    value_heads = window_values.reshape(span_tiles, TILE, HEADS, head_dim)
    scores = (
        jnp.einsum("atnd,bsnd->natbs", query_heads, key_heads, preferred_element_type=jnp.float32)
        * score_scale
    )
    scores = jnp.where(allowed[None, :, None, :, None], scores, MASKED)
    row_peak = jnp.max(scores, axis=(3, 4), keepdims=True)
    expanded = jnp.exp(scores - row_peak)
    probabilities = expanded / jnp.sum(expanded, axis=(3, 4), keepdims=True)
    rounded = probabilities.astype(jnp.bfloat16)
    attended = jnp.einsum(
        "natbs,bsnd->atnd", rounded, value_heads, preferred_element_type=jnp.float32
    )
    return (attended.reshape(row_count, model_width).astype(jnp.bfloat16), probabilities, rounded)


def attend_back(grad_attended, queries, window_keys, window_values, probabilities, rounded):
    row_count, model_width = queries.shape
    tile_count = probabilities.shape[1]
    span_tiles = probabilities.shape[3]
    head_dim = model_width // HEADS
    score_scale = head_dim ** (-0.5)
    query_heads = queries.reshape(tile_count, TILE, HEADS, head_dim)
    key_heads = window_keys.reshape(span_tiles, TILE, HEADS, head_dim)
    value_heads = window_values.reshape(span_tiles, TILE, HEADS, head_dim)
    grad_heads = grad_attended.reshape(tile_count, TILE, HEADS, head_dim)
    grad_probs = jnp.einsum(
        "atnd,bsnd->natbs", grad_heads, value_heads, preferred_element_type=jnp.float32
    )
    centre = jnp.sum(grad_probs * probabilities, axis=(3, 4), keepdims=True)
    grad_scores = (probabilities * (grad_probs - centre) * score_scale).astype(jnp.bfloat16)
    grad_queries = jnp.einsum(
        "natbs,bsnd->atnd", grad_scores, key_heads, preferred_element_type=jnp.float32
    ).reshape(row_count, model_width)
    grad_keys = jnp.einsum(
        "natbs,atnd->bsnd", grad_scores, query_heads, preferred_element_type=jnp.float32
    ).reshape(span_tiles * TILE, model_width)
    grad_values = jnp.einsum(
        "natbs,atnd->bsnd", rounded, grad_heads, preferred_element_type=jnp.float32
    ).reshape(span_tiles * TILE, model_width)
    return (grad_queries, jnp.concatenate([grad_keys, grad_values], axis=1))


def on_device(tokens, cotangent, w_qkv, w_out, norm_gain, tile_lists, tile_counts):
    own_tokens = tokens[0]
    own_grads = cotangent[0]
    row_count, model_width = own_tokens.shape
    tile_count = row_count // TILE
    tile_total = tile_lists.shape[0]
    device = lax.axis_index("node")
    own_lists = lax.dynamic_slice_in_dim(tile_lists, device * tile_count, tile_count, 0)
    own_counts = lax.dynamic_slice_in_dim(tile_counts, device * tile_count, tile_count, 0)
    allowed = tile_mask(own_lists, own_counts, (device - 1) * tile_count, tile_total)
    widened = own_tokens.astype(jnp.float32)
    inverse_rms = lax.rsqrt(jnp.mean(widened * widened, axis=-1, keepdims=True) + EPS)
    unit_rows = widened * inverse_rms
    normed = (unit_rows * norm_gain).astype(jnp.bfloat16)
    projected = jnp.dot(normed, w_qkv, preferred_element_type=jnp.float32).astype(jnp.bfloat16)
    queries = projected[:, :model_width]
    window = extended(projected[:, model_width:], (("node", 0),), row_count)
    window_keys = window[:, :model_width]
    window_values = window[:, model_width:]
    attended, probabilities, rounded = attend(queries, window_keys, window_values, allowed)
    outputs = (widened + jnp.dot(attended, w_out, preferred_element_type=jnp.float32)).astype(
        jnp.bfloat16
    )
    contract_rows = (((0,), (0,)), ((), ()))
    contract_cols = (((1,), (1,)), ((), ()))
    term_out = lax.dot_general(
        attended, own_grads, contract_rows, preferred_element_type=jnp.float32
    )
    grad_attended = lax.dot_general(
        own_grads, w_out, contract_cols, preferred_element_type=jnp.float32
    ).astype(jnp.bfloat16)
    grad_queries, grad_window = attend_back(
        grad_attended, queries, window_keys, window_values, probabilities, rounded
    )
    grad_keyvals = grad_window[row_count : 2 * row_count]
    for offset, side_index in ((-1, 0), (1, 2)):
        side_part = grad_window[side_index * row_count : (side_index + 1) * row_count]
        grad_keyvals = grad_keyvals + passed_along(
            side_part.astype(jnp.bfloat16), "node", offset
        ).astype(side_part.dtype)
    grad_projected = jnp.concatenate([grad_queries, grad_keyvals], axis=1).astype(jnp.bfloat16)
    term_qkv = lax.dot_general(
        normed, grad_projected, contract_rows, preferred_element_type=jnp.float32
    )
    grad_normed = lax.dot_general(
        grad_projected, w_qkv, contract_cols, preferred_element_type=jnp.float32
    )
    term_gain = jnp.sum(grad_normed * unit_rows, axis=0)
    grad_unit = grad_normed * norm_gain
    inner_mean = jnp.mean(grad_unit * unit_rows, axis=-1, keepdims=True)
    grad_tokens = (
        own_grads.astype(jnp.float32) + inverse_rms * (grad_unit - unit_rows * inner_mean)
    ).astype(jnp.bfloat16)
    return (outputs[None], grad_tokens[None]) + reduce_terms(term_qkv, term_out, term_gain)


def section_order(rows):
    y_size, x_size, core_size = lax.axis_size("y"), lax.axis_size("x"), lax.axis_size("core")
    shape = rows.shape
    split = rows.reshape((y_size, x_size, core_size, -1) + shape[1:])
    return jnp.moveaxis(split, (2, 1, 0), (0, 1, 2)).reshape(shape)


def exchange_sum(block, axis):
    count = lax.axis_size(axis)
    pieces = block.reshape((count, block.shape[0] // count) + block.shape[1:])
    return jnp.sum(lax.all_to_all(pieces, axis, 0, 0, tiled=False), axis=0)


def reduce_terms(term_qkv, term_out, term_gain):
    rows, model_width = term_out.shape
    gain_block = jnp.zeros((rows, 128), jnp.float32).at[:, 0].set(term_gain)
    joined = section_order(jnp.concatenate([term_qkv, term_out, gain_block], axis=1))
    for axis in ("core", "x", "y"):
        joined = exchange_sum(joined, axis)
    node_count = lax.axis_size("node")
    qkv_width = term_qkv.shape[1]
    own_rows = joined.shape[0]
    qkv_blocks = jnp.moveaxis(joined[:, :qkv_width].reshape(own_rows, node_count, -1), 1, 0)
    shared = jnp.broadcast_to(joined[None, :, qkv_width:], (node_count, own_rows, joined.shape[1] - qkv_width))
    mixed = jnp.concatenate([qkv_blocks, shared], axis=2)
    summed = jnp.sum(lax.all_to_all(mixed, "node", 0, 0, tiled=False), axis=0)
    block_width = qkv_width // node_count
    part_qkv = summed[:, :block_width]
    part_out = summed[:, block_width : block_width + model_width]
    part_gain = summed[:, block_width + model_width]
    return (part_qkv, part_out, part_gain)


def solution(mesh):
    node_size, section_size = mesh.devices.shape
    core_size = 2
    x_size = 4
    y_size = section_size // (core_size * x_size)
    fine = Mesh(mesh.devices.reshape(node_size, y_size, x_size, core_size), ("node", "y", "x", "core"))
    section = ("y", "x", "core")
    return jax.shard_map(
        on_device,
        mesh=fine,
        in_specs=(P(section, "node", None), P(section, "node", None), P(), P(), P(), P(), P()),
        out_specs=(
            P(section, "node", None),
            P(section, "node", None),
            P(section, "node"),
            P(section, None),
            P(section),
        ),
        check_vma=False,
    )
```

```python
import jax
import jax.numpy as jnp
from jax import lax
from jax.sharding import Mesh, PartitionSpec as P

HEADS = 4
TILE = 128


EPS = 1e-06
MASKED = -1000000000.0


def extended(block, sides, width):
    for axis, dim in sides:
        count = lax.axis_size(axis)
        forward = [(i, i + 1) for i in range(count - 1)]
        forward.append((count - 1, 0))
        backward = [(target, source) for source, target in forward]
        low = lax.ppermute(
            lax.slice_in_dim(block, block.shape[dim] - width, None, axis=dim), axis, forward
        )
        high = lax.ppermute(lax.slice_in_dim(block, 0, width, axis=dim), axis, backward)
        block = jnp.concatenate([low, block, high], axis=dim)
    return block


def passed_along(block, axis, distance):
    devices = range(lax.axis_size(axis))
    route = [((i - distance) % len(devices), i) for i in devices]
    return lax.ppermute(block, axis, route)


def tile_mask(own_lists, own_counts, first_tile, tile_total):
    tile_count = own_lists.shape[0]
    span_tiles = 3 * tile_count
    places = jnp.mod(own_lists - first_tile, tile_total)
    live_entries = jnp.arange(own_lists.shape[1], dtype=jnp.int32)[None, :] < own_counts[:, None]
    window_slots = jnp.arange(span_tiles, dtype=jnp.int32)
    matches = jnp.logical_and(
        places[:, :, None] == window_slots[None, None, :], live_entries[:, :, None]
    )
    return jnp.any(matches, axis=1)


def attend(queries, window_keys, window_values, allowed):
    row_count, model_width = queries.shape
    tile_count, span_tiles = allowed.shape
    head_dim = model_width // HEADS
    score_scale = head_dim ** (-0.5)
    query_heads = queries.reshape(tile_count, TILE, HEADS, head_dim)
    key_heads = window_keys.reshape(span_tiles, TILE, HEADS, head_dim)
    value_heads = window_values.reshape(span_tiles, TILE, HEADS, head_dim)
    scores = (
        jnp.einsum("atnd,bsnd->natbs", query_heads, key_heads, preferred_element_type=jnp.float32)
        * score_scale
    )
    scores = jnp.where(allowed[None, :, None, :, None], scores, MASKED)
    row_peak = jnp.max(scores, axis=(3, 4), keepdims=True)
    expanded = jnp.exp(scores - row_peak)
    probabilities = expanded / jnp.sum(expanded, axis=(3, 4), keepdims=True)
    rounded = probabilities.astype(jnp.bfloat16)
    attended = jnp.einsum(
        "natbs,bsnd->atnd", rounded, value_heads, preferred_element_type=jnp.float32
    )
    return (attended.reshape(row_count, model_width).astype(jnp.bfloat16), probabilities, rounded)


def attend_back(grad_attended, queries, window_keys, window_values, probabilities, rounded):
    row_count, model_width = queries.shape
    tile_count = probabilities.shape[1]
    span_tiles = probabilities.shape[3]
    head_dim = model_width // HEADS
    score_scale = head_dim ** (-0.5)
    query_heads = queries.reshape(tile_count, TILE, HEADS, head_dim)
    key_heads = window_keys.reshape(span_tiles, TILE, HEADS, head_dim)
    value_heads = window_values.reshape(span_tiles, TILE, HEADS, head_dim)
    grad_heads = grad_attended.reshape(tile_count, TILE, HEADS, head_dim)
    grad_probs = jnp.einsum(
        "atnd,bsnd->natbs", grad_heads, value_heads, preferred_element_type=jnp.float32
    )
    centre = jnp.sum(grad_probs * probabilities, axis=(3, 4), keepdims=True)
    grad_scores = (probabilities * (grad_probs - centre) * score_scale).astype(jnp.bfloat16)
    grad_queries = jnp.einsum(
        "natbs,bsnd->atnd", grad_scores, key_heads, preferred_element_type=jnp.float32
    ).reshape(row_count, model_width)
    grad_keys = jnp.einsum(
        "natbs,atnd->bsnd", grad_scores, query_heads, preferred_element_type=jnp.float32
    ).reshape(span_tiles * TILE, model_width)
    grad_values = jnp.einsum(
        "natbs,atnd->bsnd", rounded, grad_heads, preferred_element_type=jnp.float32
    ).reshape(span_tiles * TILE, model_width)
    return (grad_queries, jnp.concatenate([grad_keys, grad_values], axis=1))


def on_device(tokens, cotangent, w_qkv, w_out, norm_gain, tile_lists, tile_counts):
    own_tokens = tokens[0]
    own_grads = cotangent[0]
    row_count, model_width = own_tokens.shape
    tile_count = row_count // TILE
    tile_total = tile_lists.shape[0]
    device = lax.axis_index("node")
    own_lists = lax.dynamic_slice_in_dim(tile_lists, device * tile_count, tile_count, 0)
    own_counts = lax.dynamic_slice_in_dim(tile_counts, device * tile_count, tile_count, 0)
    allowed = tile_mask(own_lists, own_counts, (device - 1) * tile_count, tile_total)
    widened = own_tokens.astype(jnp.float32)
    inverse_rms = lax.rsqrt(jnp.mean(widened * widened, axis=-1, keepdims=True) + EPS)
    unit_rows = widened * inverse_rms
    normed = (unit_rows * norm_gain).astype(jnp.bfloat16)
    projected = jnp.dot(normed, w_qkv, preferred_element_type=jnp.float32).astype(jnp.bfloat16)
    queries = projected[:, :model_width]
    window = extended(projected[:, model_width:], (("node", 0),), row_count)
    window_keys = window[:, :model_width]
    window_values = window[:, model_width:]
    attended, probabilities, rounded = attend(queries, window_keys, window_values, allowed)
    outputs = (widened + jnp.dot(attended, w_out, preferred_element_type=jnp.float32)).astype(
        jnp.bfloat16
    )
    contract_rows = (((0,), (0,)), ((), ()))
    contract_cols = (((1,), (1,)), ((), ()))
    term_out = lax.dot_general(
        attended, own_grads, contract_rows, preferred_element_type=jnp.float32
    )
    grad_attended = lax.dot_general(
        own_grads, w_out, contract_cols, preferred_element_type=jnp.float32
    ).astype(jnp.bfloat16)
    grad_queries, grad_window = attend_back(
        grad_attended, queries, window_keys, window_values, probabilities, rounded
    )
    grad_keyvals = grad_window[row_count : 2 * row_count]
    for offset, side_index in ((-1, 0), (1, 2)):
        side_part = grad_window[side_index * row_count : (side_index + 1) * row_count]
        grad_keyvals = grad_keyvals + passed_along(
            side_part.astype(jnp.bfloat16), "node", offset
        ).astype(side_part.dtype)
    grad_projected = jnp.concatenate([grad_queries, grad_keyvals], axis=1).astype(jnp.bfloat16)
    term_qkv = lax.dot_general(
        normed, grad_projected, contract_rows, preferred_element_type=jnp.float32
    )
    grad_normed = lax.dot_general(
        grad_projected, w_qkv, contract_cols, preferred_element_type=jnp.float32
    )
    term_gain = jnp.sum(grad_normed * unit_rows, axis=0)
    grad_unit = grad_normed * norm_gain
    inner_mean = jnp.mean(grad_unit * unit_rows, axis=-1, keepdims=True)
    grad_tokens = (
        own_grads.astype(jnp.float32) + inverse_rms * (grad_unit - unit_rows * inner_mean)
    ).astype(jnp.bfloat16)
    return (outputs[None], grad_tokens[None]) + reduce_terms(term_qkv, term_out, term_gain)


def section_order(rows):
    y_size, x_size, core_size = lax.axis_size("y"), lax.axis_size("x"), lax.axis_size("core")
    shape = rows.shape
    split = rows.reshape((y_size, x_size, core_size, -1) + shape[1:])
    return jnp.moveaxis(split, (2, 1, 0), (0, 1, 2)).reshape(shape)


def exchange_sum(block, axis):
    count = lax.axis_size(axis)
    pieces = block.reshape((count, block.shape[0] // count) + block.shape[1:])
    return wide_sum(lax.all_to_all(pieces.astype(jnp.bfloat16), axis, 0, 0, tiled=False))


def wide_sum(pieces):
    return jnp.sum(pieces.astype(jnp.float32), axis=0)


def reduce_terms(term_qkv, term_out, term_gain):
    rows, model_width = term_out.shape
    gain_block = jnp.zeros((rows, 128), jnp.float32).at[:, 0].set(term_gain)
    joined = section_order(jnp.concatenate([term_qkv, term_out, gain_block], axis=1))
    for axis in ("core", "x", "y"):
        joined = exchange_sum(joined, axis)
    node_count = lax.axis_size("node")
    qkv_width = term_qkv.shape[1]
    own_rows = joined.shape[0]
    qkv_blocks = jnp.moveaxis(joined[:, :qkv_width].reshape(own_rows, node_count, -1), 1, 0)
    shared = jnp.broadcast_to(joined[None, :, qkv_width:], (node_count, own_rows, joined.shape[1] - qkv_width))
    mixed = jnp.concatenate([qkv_blocks, shared], axis=2)
    summed = wide_sum(lax.all_to_all(mixed.astype(jnp.bfloat16), "node", 0, 0, tiled=False))
    block_width = qkv_width // node_count
    part_qkv = summed[:, :block_width]
    part_out = summed[:, block_width : block_width + model_width]
    part_gain = summed[:, block_width + model_width]
    return (part_qkv, part_out, part_gain)


def solution(mesh):
    node_size, section_size = mesh.devices.shape
    core_size = 2
    x_size = 4
    y_size = section_size // (core_size * x_size)
    fine = Mesh(mesh.devices.reshape(node_size, y_size, x_size, core_size), ("node", "y", "x", "core"))
    section = ("y", "x", "core")
    return jax.shard_map(
        on_device,
        mesh=fine,
        in_specs=(P(section, "node", None), P(section, "node", None), P(), P(), P(), P(), P()),
        out_specs=(
            P(section, "node", None),
            P(section, "node", None),
            P(section, "node"),
            P(section, None),
            P(section),
        ),
        check_vma=False,
    )
```

```python
import jax
import jax.numpy as jnp
from jax import lax
from jax.experimental import pallas as pl
from jax.sharding import Mesh, PartitionSpec as P

HEADS = 4
TILE = 128


EPS = 1e-06
MASKED = -1000000000.0


def extended(block, sides, width):
    for axis, dim in sides:
        count = lax.axis_size(axis)
        forward = [(i, i + 1) for i in range(count - 1)]
        forward.append((count - 1, 0))
        backward = [(target, source) for source, target in forward]
        low = lax.ppermute(
            lax.slice_in_dim(block, block.shape[dim] - width, None, axis=dim), axis, forward
        )
        high = lax.ppermute(lax.slice_in_dim(block, 0, width, axis=dim), axis, backward)
        block = jnp.concatenate([low, block, high], axis=dim)
    return block


def passed_along(block, axis, distance):
    devices = range(lax.axis_size(axis))
    route = [((i - distance) % len(devices), i) for i in devices]
    return lax.ppermute(block, axis, route)


def tile_mask(own_lists, own_counts, first_tile, tile_total):
    tile_count = own_lists.shape[0]
    span_tiles = 3 * tile_count
    places = jnp.mod(own_lists - first_tile, tile_total)
    live_entries = jnp.arange(own_lists.shape[1], dtype=jnp.int32)[None, :] < own_counts[:, None]
    window_slots = jnp.arange(span_tiles, dtype=jnp.int32)
    matches = jnp.logical_and(
        places[:, :, None] == window_slots[None, None, :], live_entries[:, :, None]
    )
    return jnp.any(matches, axis=1)


def attention_kernel(mask_ref, q_ref, k_ref, v_ref, ga_ref, att_ref, gq_ref, gk_ref, gv_ref):
    head_dim = q_ref.shape[1]
    score_scale = head_dim ** (-0.5)
    keys = k_ref[...]
    values = v_ref[...]
    nt = (((1,), (1,)), ((), ()))
    tn = (((0,), (0,)), ((), ()))
    grad_keys = jnp.zeros(gk_ref.shape, jnp.float32)
    grad_values = jnp.zeros(gv_ref.shape, jnp.float32)
    for tile in range(q_ref.shape[0] // TILE):
        rows = slice(tile * TILE, (tile + 1) * TILE)
        queries = q_ref[rows, :]
        grads = ga_ref[rows, :]
        keep = mask_ref[tile : tile + 1, :] > 0.5
        scores = lax.dot_general(queries, keys, nt, preferred_element_type=jnp.float32) * score_scale
        scores = jnp.where(keep, scores, MASKED)
        peak = jnp.max(scores, axis=1, keepdims=True)
        expanded = jnp.exp(scores - peak)
        probabilities = expanded / jnp.sum(expanded, axis=1, keepdims=True)
        rounded = probabilities.astype(jnp.bfloat16)
        att_ref[rows, :] = jnp.dot(rounded, values, preferred_element_type=jnp.float32).astype(att_ref.dtype)
        grad_probs = lax.dot_general(grads, values, nt, preferred_element_type=jnp.float32)
        centre = jnp.sum(grad_probs * probabilities, axis=1, keepdims=True)
        grad_scores = (probabilities * (grad_probs - centre) * score_scale).astype(jnp.bfloat16)
        gq_ref[rows, :] = jnp.dot(grad_scores, keys, preferred_element_type=jnp.float32)
        grad_keys = grad_keys + lax.dot_general(grad_scores, queries, tn, preferred_element_type=jnp.float32)
        grad_values = grad_values + lax.dot_general(rounded, grads, tn, preferred_element_type=jnp.float32)
    gk_ref[...] = grad_keys
    gv_ref[...] = grad_values


def fused_attention(keep_rows, queries, window_keys, window_values, grad_attended, heads):
    rows, width = queries.shape
    span = window_keys.shape[0]
    head_dim = width // heads
    q_spec = pl.BlockSpec((rows, head_dim), lambda h: (0, h))
    w_spec = pl.BlockSpec((span, head_dim), lambda h: (0, h))
    m_spec = pl.BlockSpec(keep_rows.shape, lambda h: (0, 0))
    flops = 12 * rows * span * width
    cost = pl.CostEstimate(flops=flops, transcendentals=rows * span * heads,
                           bytes_accessed=2 * (2 * rows * width + 2 * span * width) + 4 * (rows * width + 2 * span * width) + 2 * rows * width)
    return pl.pallas_call(
        attention_kernel,
        grid=(heads,),
        in_specs=[m_spec, q_spec, w_spec, w_spec, q_spec],
        out_specs=[q_spec, q_spec, w_spec, w_spec],
        out_shape=[
            jax.ShapeDtypeStruct((rows, width), jnp.bfloat16),
            jax.ShapeDtypeStruct((rows, width), jnp.float32),
            jax.ShapeDtypeStruct((span, width), jnp.float32),
            jax.ShapeDtypeStruct((span, width), jnp.float32),
        ],
        cost_estimate=cost,
    )(keep_rows, queries, window_keys, window_values, grad_attended)


def on_device(tokens, cotangent, w_qkv, w_out, norm_gain, tile_lists, tile_counts):
    own_tokens = tokens[0]
    own_grads = cotangent[0]
    row_count, model_width = own_tokens.shape
    tile_count = row_count // TILE
    tile_total = tile_lists.shape[0]
    device = lax.axis_index("node")
    own_lists = lax.dynamic_slice_in_dim(tile_lists, device * tile_count, tile_count, 0)
    own_counts = lax.dynamic_slice_in_dim(tile_counts, device * tile_count, tile_count, 0)
    allowed = tile_mask(own_lists, own_counts, (device - 1) * tile_count, tile_total)
    widened = own_tokens.astype(jnp.float32)
    inverse_rms = lax.rsqrt(jnp.mean(widened * widened, axis=-1, keepdims=True) + EPS)
    unit_rows = widened * inverse_rms
    normed = (unit_rows * norm_gain).astype(jnp.bfloat16)
    projected = jnp.dot(normed, w_qkv, preferred_element_type=jnp.float32).astype(jnp.bfloat16)
    queries = projected[:, :model_width]
    window = extended(projected[:, model_width:], (("node", 0),), row_count)
    window_keys = window[:, :model_width]
    window_values = window[:, model_width:]
    contract_rows = (((0,), (0,)), ((), ()))
    contract_cols = (((1,), (1,)), ((), ()))
    grad_attended = lax.dot_general(
        own_grads, w_out, contract_cols, preferred_element_type=jnp.float32
    ).astype(jnp.bfloat16)
    keep_rows = jnp.zeros((8, window_keys.shape[0]), jnp.float32)
    keep_rows = keep_rows.at[:tile_count].set(jnp.repeat(allowed, TILE, axis=1).astype(jnp.float32))
    attended, grad_queries, grad_keys, grad_values = fused_attention(
        keep_rows, queries, window_keys, window_values, grad_attended, HEADS
    )
    grad_window = jnp.concatenate([grad_keys, grad_values], axis=1)
    outputs = (widened + jnp.dot(attended, w_out, preferred_element_type=jnp.float32)).astype(
        jnp.bfloat16
    )
    term_out = lax.dot_general(
        attended, own_grads, contract_rows, preferred_element_type=jnp.float32
    )
    grad_keyvals = grad_window[row_count : 2 * row_count]
    for offset, side_index in ((-1, 0), (1, 2)):
        side_part = grad_window[side_index * row_count : (side_index + 1) * row_count]
        grad_keyvals = grad_keyvals + passed_along(
            side_part.astype(jnp.bfloat16), "node", offset
        ).astype(side_part.dtype)
    grad_projected = jnp.concatenate([grad_queries, grad_keyvals], axis=1).astype(jnp.bfloat16)
    term_qkv = lax.dot_general(
        normed, grad_projected, contract_rows, preferred_element_type=jnp.float32
    )
    grad_normed = lax.dot_general(
        grad_projected, w_qkv, contract_cols, preferred_element_type=jnp.float32
    )
    term_gain = jnp.sum(grad_normed * unit_rows, axis=0)
    grad_unit = grad_normed * norm_gain
    inner_mean = jnp.mean(grad_unit * unit_rows, axis=-1, keepdims=True)
    grad_tokens = (
        own_grads.astype(jnp.float32) + inverse_rms * (grad_unit - unit_rows * inner_mean)
    ).astype(jnp.bfloat16)
    return (outputs[None], grad_tokens[None]) + reduce_terms(term_qkv, term_out, term_gain)


def section_order(rows):
    y_size, x_size, core_size = lax.axis_size("y"), lax.axis_size("x"), lax.axis_size("core")
    shape = rows.shape
    split = rows.reshape((y_size, x_size, core_size, -1) + shape[1:])
    return jnp.moveaxis(split, (2, 1, 0), (0, 1, 2)).reshape(shape)


def exchange_sum(block, axis):
    count = lax.axis_size(axis)
    pieces = block.reshape((count, block.shape[0] // count) + block.shape[1:])
    return wide_sum(lax.all_to_all(pieces.astype(jnp.bfloat16), axis, 0, 0, tiled=False))


def wide_sum(pieces):
    return jnp.sum(pieces.astype(jnp.float32), axis=0)


def reduce_terms(term_qkv, term_out, term_gain):
    rows, model_width = term_out.shape
    gain_block = jnp.zeros((rows, 128), jnp.float32).at[:, 0].set(term_gain)
    joined = section_order(jnp.concatenate([term_qkv, term_out, gain_block], axis=1))
    for axis in ("core", "x", "y"):
        joined = exchange_sum(joined, axis)
    node_count = lax.axis_size("node")
    qkv_width = term_qkv.shape[1]
    own_rows = joined.shape[0]
    qkv_blocks = jnp.moveaxis(joined[:, :qkv_width].reshape(own_rows, node_count, -1), 1, 0)
    shared = jnp.broadcast_to(joined[None, :, qkv_width:], (node_count, own_rows, joined.shape[1] - qkv_width))
    mixed = jnp.concatenate([qkv_blocks, shared], axis=2)
    summed = wide_sum(lax.all_to_all(mixed.astype(jnp.bfloat16), "node", 0, 0, tiled=False))
    block_width = qkv_width // node_count
    part_qkv = summed[:, :block_width]
    part_out = summed[:, block_width : block_width + model_width]
    part_gain = summed[:, block_width + model_width]
    return (part_qkv, part_out, part_gain)


def solution(mesh):
    node_size, section_size = mesh.devices.shape
    core_size = 2
    x_size = 4
    y_size = section_size // (core_size * x_size)
    fine = Mesh(mesh.devices.reshape(node_size, y_size, x_size, core_size), ("node", "y", "x", "core"))
    section = ("y", "x", "core")
    return jax.shard_map(
        on_device,
        mesh=fine,
        in_specs=(P(section, "node", None), P(section, "node", None), P(), P(), P(), P(), P()),
        out_specs=(
            P(section, "node", None),
            P(section, "node", None),
            P(section, "node"),
            P(section, None),
            P(section),
        ),
        check_vma=False,
    )
```

```python
import jax
import jax.numpy as jnp
from jax import lax
from jax.experimental import pallas as pl
from jax.sharding import Mesh, PartitionSpec as P

HEADS = 4
TILE = 128


EPS = 1e-06
MASKED = -1000000000.0


def extended(block, sides, width):
    for axis, dim in sides:
        count = lax.axis_size(axis)
        forward = [(i, i + 1) for i in range(count - 1)]
        forward.append((count - 1, 0))
        backward = [(target, source) for source, target in forward]
        low = lax.ppermute(
            lax.slice_in_dim(block, block.shape[dim] - width, None, axis=dim), axis, forward
        )
        high = lax.ppermute(lax.slice_in_dim(block, 0, width, axis=dim), axis, backward)
        block = jnp.concatenate([low, block, high], axis=dim)
    return block


def passed_along(block, axis, distance):
    devices = range(lax.axis_size(axis))
    route = [((i - distance) % len(devices), i) for i in devices]
    return lax.ppermute(block, axis, route)


def tile_mask(own_lists, own_counts, first_tile, tile_total):
    tile_count = own_lists.shape[0]
    span_tiles = 3 * tile_count
    places = jnp.mod(own_lists - first_tile, tile_total)
    live_entries = jnp.arange(own_lists.shape[1], dtype=jnp.int32)[None, :] < own_counts[:, None]
    window_slots = jnp.arange(span_tiles, dtype=jnp.int32)
    matches = jnp.logical_and(
        places[:, :, None] == window_slots[None, None, :], live_entries[:, :, None]
    )
    return jnp.any(matches, axis=1)


def attention_kernel(mask_ref, q_ref, k_ref, v_ref, ga_ref, att_ref, gq_ref, gk_ref, gv_ref):
    head_dim = q_ref.shape[1]
    score_scale = head_dim ** (-0.5)
    keys = k_ref[...]
    values = v_ref[...]
    nt = (((1,), (1,)), ((), ()))
    tn = (((0,), (0,)), ((), ()))
    grad_keys = jnp.zeros(gk_ref.shape, jnp.float32)
    grad_values = jnp.zeros(gv_ref.shape, jnp.float32)
    for tile in range(q_ref.shape[0] // TILE):
        rows = slice(tile * TILE, (tile + 1) * TILE)
        queries = q_ref[rows, :]
        grads = ga_ref[rows, :]
        keep = mask_ref[tile : tile + 1, :] > 0.5
        scores = lax.dot_general(queries, keys, nt, preferred_element_type=jnp.float32) * score_scale
        scores = jnp.where(keep, scores, MASKED)
        peak = jnp.max(scores, axis=1, keepdims=True)
        expanded = jnp.exp(scores - peak)
        probabilities = expanded / jnp.sum(expanded, axis=1, keepdims=True)
        rounded = probabilities.astype(jnp.bfloat16)
        att_ref[rows, :] = jnp.dot(rounded, values, preferred_element_type=jnp.float32).astype(att_ref.dtype)
        grad_probs = lax.dot_general(grads, values, nt, preferred_element_type=jnp.float32)
        centre = jnp.sum(grad_probs * probabilities, axis=1, keepdims=True)
        grad_scores = (probabilities * (grad_probs - centre) * score_scale).astype(jnp.bfloat16)
        gq_ref[rows, :] = jnp.dot(grad_scores, keys, preferred_element_type=jnp.float32)
        grad_keys = grad_keys + lax.dot_general(grad_scores, queries, tn, preferred_element_type=jnp.float32)
        grad_values = grad_values + lax.dot_general(rounded, grads, tn, preferred_element_type=jnp.float32)
    gk_ref[...] = grad_keys
    gv_ref[...] = grad_values


def fused_attention(keep_rows, queries, window_keys, window_values, grad_attended, heads):
    rows, width = queries.shape
    span = window_keys.shape[0]
    head_dim = width // heads
    q_spec = pl.BlockSpec((rows, head_dim), lambda h: (0, h))
    w_spec = pl.BlockSpec((span, head_dim), lambda h: (0, h))
    m_spec = pl.BlockSpec(keep_rows.shape, lambda h: (0, 0))
    flops = 12 * rows * span * width
    cost = pl.CostEstimate(flops=flops, transcendentals=rows * span * heads,
                           bytes_accessed=2 * (2 * rows * width + 2 * span * width) + 4 * (rows * width + 2 * span * width) + 2 * rows * width)
    return pl.pallas_call(
        attention_kernel,
        grid=(heads,),
        in_specs=[m_spec, q_spec, w_spec, w_spec, q_spec],
        out_specs=[q_spec, q_spec, w_spec, w_spec],
        out_shape=[
            jax.ShapeDtypeStruct((rows, width), jnp.bfloat16),
            jax.ShapeDtypeStruct((rows, width), jnp.float32),
            jax.ShapeDtypeStruct((span, width), jnp.float32),
            jax.ShapeDtypeStruct((span, width), jnp.float32),
        ],
        cost_estimate=cost,
    )(keep_rows, queries, window_keys, window_values, grad_attended)


def on_device(tokens, cotangent, w_qkv, w_out, norm_gain, tile_lists, tile_counts):
    own_tokens = tokens[0]
    own_grads = cotangent[0]
    row_count, model_width = own_tokens.shape
    tile_count = row_count // TILE
    tile_total = tile_lists.shape[0]
    device = lax.axis_index("node")
    own_lists = lax.dynamic_slice_in_dim(tile_lists, device * tile_count, tile_count, 0)
    own_counts = lax.dynamic_slice_in_dim(tile_counts, device * tile_count, tile_count, 0)
    allowed = tile_mask(own_lists, own_counts, (device - 1) * tile_count, tile_total)
    widened = own_tokens.astype(jnp.float32)
    inverse_rms = lax.rsqrt(jnp.mean(widened * widened, axis=-1, keepdims=True) + EPS)
    unit_rows = widened * inverse_rms
    normed = (unit_rows * norm_gain).astype(jnp.bfloat16)
    projected = jnp.dot(normed, w_qkv, preferred_element_type=jnp.float32).astype(jnp.bfloat16)
    queries = projected[:, :model_width]
    window = extended(projected[:, model_width:], (("node", 0),), row_count)
    window_keys = window[:, :model_width]
    window_values = window[:, model_width:]
    contract_rows = (((0,), (0,)), ((), ()))
    contract_cols = (((1,), (1,)), ((), ()))
    grad_attended = lax.dot_general(
        own_grads, w_out, contract_cols, preferred_element_type=jnp.float32
    ).astype(jnp.bfloat16)
    keep_rows = jnp.zeros((8, window_keys.shape[0]), jnp.float32)
    keep_rows = keep_rows.at[:tile_count].set(jnp.repeat(allowed, TILE, axis=1).astype(jnp.float32))
    attended, grad_queries, grad_keys, grad_values = fused_attention(
        keep_rows, queries, window_keys, window_values, grad_attended, HEADS
    )
    grad_window = jnp.concatenate([grad_keys, grad_values], axis=1)
    outputs = (widened + jnp.dot(attended, w_out, preferred_element_type=jnp.float32)).astype(
        jnp.bfloat16
    )
    term_out = lax.dot_general(
        attended, own_grads, contract_rows, preferred_element_type=jnp.float32
    )
    grad_q = grad_queries.astype(jnp.bfloat16)
    term_q = lax.dot_general(normed, grad_q, contract_rows, preferred_element_type=jnp.float32)
    early = section_sum(jnp.concatenate([term_q, term_out], axis=1))
    grad_keyvals = grad_window[row_count : 2 * row_count]
    for offset, side_index in ((-1, 0), (1, 2)):
        side_part = grad_window[side_index * row_count : (side_index + 1) * row_count]
        grad_keyvals = grad_keyvals + passed_along(
            side_part.astype(jnp.bfloat16), "node", offset
        ).astype(side_part.dtype)
    grad_kv = grad_keyvals.astype(jnp.bfloat16)
    term_kv = lax.dot_general(normed, grad_kv, contract_rows, preferred_element_type=jnp.float32)
    grad_normed = lax.dot_general(
        grad_q, w_qkv[:, :model_width], contract_cols, preferred_element_type=jnp.float32
    ) + lax.dot_general(
        grad_kv, w_qkv[:, model_width:], contract_cols, preferred_element_type=jnp.float32
    )
    term_gain = jnp.sum(grad_normed * unit_rows, axis=0)
    grad_unit = grad_normed * norm_gain
    inner_mean = jnp.mean(grad_unit * unit_rows, axis=-1, keepdims=True)
    grad_tokens = (
        own_grads.astype(jnp.float32) + inverse_rms * (grad_unit - unit_rows * inner_mean)
    ).astype(jnp.bfloat16)
    gain_block = jnp.zeros((model_width, 128), jnp.float32).at[:, 0].set(term_gain)
    late = section_sum(jnp.concatenate([term_kv, gain_block], axis=1))
    return (outputs[None], grad_tokens[None]) + node_sum(early, late, model_width)


def section_order(rows):
    y_size, x_size, core_size = lax.axis_size("y"), lax.axis_size("x"), lax.axis_size("core")
    shape = rows.shape
    split = rows.reshape((y_size, x_size, core_size, -1) + shape[1:])
    return jnp.moveaxis(split, (2, 1, 0), (0, 1, 2)).reshape(shape)


def exchange_sum(block, axis):
    count = lax.axis_size(axis)
    pieces = block.reshape((count, block.shape[0] // count) + block.shape[1:])
    return wide_sum(lax.all_to_all(pieces.astype(jnp.bfloat16), axis, 0, 0, tiled=False))


def wide_sum(pieces):
    return jnp.sum(pieces.astype(jnp.float32), axis=0)


def section_sum(term):
    joined = section_order(term)
    for axis in ("core", "x", "y"):
        joined = exchange_sum(joined, axis)
    return joined


def node_sum(early, late, model_width):
    node_count = lax.axis_size("node")
    own_rows = early.shape[0]
    qkv = jnp.concatenate([early[:, :model_width], late[:, : 2 * model_width]], axis=1)
    rest = jnp.concatenate([early[:, model_width:], late[:, 2 * model_width :]], axis=1)
    qkv_blocks = jnp.moveaxis(qkv.reshape(own_rows, node_count, -1), 1, 0)
    shared = jnp.broadcast_to(rest[None], (node_count,) + rest.shape)
    mixed = jnp.concatenate([qkv_blocks, shared], axis=2)
    summed = wide_sum(lax.all_to_all(mixed.astype(jnp.bfloat16), "node", 0, 0, tiled=False))
    block_width = qkv.shape[1] // node_count
    part_qkv = summed[:, :block_width]
    part_out = summed[:, block_width : block_width + model_width]
    part_gain = summed[:, block_width + model_width]
    return (part_qkv, part_out, part_gain)


def solution(mesh):
    node_size, section_size = mesh.devices.shape
    core_size = 2
    x_size = 4
    y_size = section_size // (core_size * x_size)
    fine = Mesh(mesh.devices.reshape(node_size, y_size, x_size, core_size), ("node", "y", "x", "core"))
    section = ("y", "x", "core")
    return jax.shard_map(
        on_device,
        mesh=fine,
        in_specs=(P(section, "node", None), P(section, "node", None), P(), P(), P(), P(), P()),
        out_specs=(
            P(section, "node", None),
            P(section, "node", None),
            P(section, "node"),
            P(section, None),
            P(section),
        ),
        check_vma=False,
    )
```

```python
import jax
import jax.numpy as jnp
from jax import lax
from jax.experimental import pallas as pl
from jax.sharding import Mesh, PartitionSpec as P

HEADS = 4
TILE = 128


EPS = 1e-06
MASKED = -1000000000.0


def extended(block, sides, width):
    for axis, dim in sides:
        count = lax.axis_size(axis)
        forward = [(i, i + 1) for i in range(count - 1)]
        forward.append((count - 1, 0))
        backward = [(target, source) for source, target in forward]
        low = lax.ppermute(
            lax.slice_in_dim(block, block.shape[dim] - width, None, axis=dim), axis, forward
        )
        high = lax.ppermute(lax.slice_in_dim(block, 0, width, axis=dim), axis, backward)
        block = jnp.concatenate([low, block, high], axis=dim)
    return block


def passed_along(block, axis, distance):
    devices = range(lax.axis_size(axis))
    route = [((i - distance) % len(devices), i) for i in devices]
    return lax.ppermute(block, axis, route)


def tile_mask(own_lists, own_counts, first_tile, tile_total):
    tile_count = own_lists.shape[0]
    span_tiles = 3 * tile_count
    places = jnp.mod(own_lists - first_tile, tile_total)
    live_entries = jnp.arange(own_lists.shape[1], dtype=jnp.int32)[None, :] < own_counts[:, None]
    window_slots = jnp.arange(span_tiles, dtype=jnp.int32)
    matches = jnp.logical_and(
        places[:, :, None] == window_slots[None, None, :], live_entries[:, :, None]
    )
    return jnp.any(matches, axis=1)


def attention_kernel(mask_ref, q_ref, k_ref, v_ref, ga_ref, att_ref, gq_ref, gk_ref, gv_ref):
    head_dim = q_ref.shape[1]
    score_scale = head_dim ** (-0.5)
    keys = k_ref[...]
    values = v_ref[...]
    nt = (((1,), (1,)), ((), ()))
    tn = (((0,), (0,)), ((), ()))
    grad_keys = jnp.zeros(gk_ref.shape, jnp.float32)
    grad_values = jnp.zeros(gv_ref.shape, jnp.float32)
    for tile in range(q_ref.shape[0] // TILE):
        rows = slice(tile * TILE, (tile + 1) * TILE)
        queries = q_ref[rows, :]
        grads = ga_ref[rows, :]
        keep = mask_ref[tile : tile + 1, :] > 0.5
        scores = lax.dot_general(queries, keys, nt, preferred_element_type=jnp.float32) * score_scale
        scores = jnp.where(keep, scores, MASKED)
        peak = jnp.max(scores, axis=1, keepdims=True)
        expanded = jnp.exp(scores - peak)
        probabilities = expanded / jnp.sum(expanded, axis=1, keepdims=True)
        rounded = probabilities.astype(jnp.bfloat16)
        att_ref[rows, :] = jnp.dot(rounded, values, preferred_element_type=jnp.float32).astype(att_ref.dtype)
        grad_probs = lax.dot_general(grads, values, nt, preferred_element_type=jnp.float32)
        centre = jnp.sum(grad_probs * probabilities, axis=1, keepdims=True)
        grad_scores = (probabilities * (grad_probs - centre) * score_scale).astype(jnp.bfloat16)
        gq_ref[rows, :] = jnp.dot(grad_scores, keys, preferred_element_type=jnp.float32)
        grad_keys = grad_keys + lax.dot_general(grad_scores, queries, tn, preferred_element_type=jnp.float32)
        grad_values = grad_values + lax.dot_general(rounded, grads, tn, preferred_element_type=jnp.float32)
    gk_ref[...] = grad_keys
    gv_ref[...] = grad_values


def fused_attention(keep_rows, queries, window_keys, window_values, grad_attended, heads):
    rows, width = queries.shape
    span = window_keys.shape[0]
    head_dim = width // heads
    q_spec = pl.BlockSpec((rows, head_dim), lambda h: (0, h))
    w_spec = pl.BlockSpec((span, head_dim), lambda h: (0, h))
    m_spec = pl.BlockSpec(keep_rows.shape, lambda h: (0, 0))
    flops = 12 * rows * span * width
    cost = pl.CostEstimate(flops=flops, transcendentals=rows * span * heads,
                           bytes_accessed=2 * (2 * rows * width + 2 * span * width) + 4 * (rows * width + 2 * span * width) + 2 * rows * width)
    return pl.pallas_call(
        attention_kernel,
        grid=(heads,),
        in_specs=[m_spec, q_spec, w_spec, w_spec, q_spec],
        out_specs=[q_spec, q_spec, w_spec, w_spec],
        out_shape=[
            jax.ShapeDtypeStruct((rows, width), jnp.bfloat16),
            jax.ShapeDtypeStruct((rows, width), jnp.float32),
            jax.ShapeDtypeStruct((span, width), jnp.float32),
            jax.ShapeDtypeStruct((span, width), jnp.float32),
        ],
        cost_estimate=cost,
    )(keep_rows, queries, window_keys, window_values, grad_attended)


def on_device(tokens, cotangent, w_qkv, w_out, norm_gain, tile_lists, tile_counts):
    own_tokens = tokens[0]
    own_grads = cotangent[0]
    row_count, model_width = own_tokens.shape
    tile_count = row_count // TILE
    tile_total = tile_lists.shape[0]
    device = lax.axis_index("node")
    own_lists = lax.dynamic_slice_in_dim(tile_lists, device * tile_count, tile_count, 0)
    own_counts = lax.dynamic_slice_in_dim(tile_counts, device * tile_count, tile_count, 0)
    allowed = tile_mask(own_lists, own_counts, (device - 1) * tile_count, tile_total)
    widened = own_tokens.astype(jnp.float32)
    inverse_rms = lax.rsqrt(jnp.mean(widened * widened, axis=-1, keepdims=True) + EPS)
    unit_rows = widened * inverse_rms
    normed = (unit_rows * norm_gain).astype(jnp.bfloat16)
    projected = jnp.dot(normed, w_qkv, preferred_element_type=jnp.float32).astype(jnp.bfloat16)
    queries = projected[:, :model_width]
    window = extended(projected[:, model_width:], (("node", 0),), row_count)
    window_keys = window[:, :model_width]
    window_values = window[:, model_width:]
    contract_rows = (((0,), (0,)), ((), ()))
    contract_cols = (((1,), (1,)), ((), ()))
    grad_attended = lax.dot_general(
        own_grads, w_out, contract_cols, preferred_element_type=jnp.float32
    ).astype(jnp.bfloat16)
    keep_rows = jnp.zeros((8, window_keys.shape[0]), jnp.float32)
    keep_rows = keep_rows.at[:tile_count].set(jnp.repeat(allowed, TILE, axis=1).astype(jnp.float32))
    attended, grad_queries, grad_keys, grad_values = fused_attention(
        keep_rows, queries, window_keys, window_values, grad_attended, HEADS
    )
    grad_window = jnp.concatenate([grad_keys, grad_values], axis=1)
    outputs = (widened + jnp.dot(attended, w_out, preferred_element_type=jnp.float32)).astype(
        jnp.bfloat16
    )
    term_out = lax.dot_general(
        attended, own_grads, contract_rows, preferred_element_type=jnp.float32
    )
    grad_keyvals = grad_window[row_count : 2 * row_count]
    for offset, side_index in ((-1, 0), (1, 2)):
        side_part = grad_window[side_index * row_count : (side_index + 1) * row_count]
        grad_keyvals = grad_keyvals + passed_along(
            side_part.astype(jnp.bfloat16), "node", offset
        ).astype(side_part.dtype)
    grad_projected = jnp.concatenate([grad_queries, grad_keyvals], axis=1).astype(jnp.bfloat16)
    term_qkv = lax.dot_general(
        normed, grad_projected, contract_rows, preferred_element_type=jnp.float32
    )
    grad_normed = lax.dot_general(
        grad_projected, w_qkv, contract_cols, preferred_element_type=jnp.float32
    )
    term_gain = jnp.sum(grad_normed * unit_rows, axis=0)
    grad_unit = grad_normed * norm_gain
    inner_mean = jnp.mean(grad_unit * unit_rows, axis=-1, keepdims=True)
    grad_tokens = (
        own_grads.astype(jnp.float32) + inverse_rms * (grad_unit - unit_rows * inner_mean)
    ).astype(jnp.bfloat16)
    return (outputs[None], grad_tokens[None]) + reduce_terms(term_qkv, term_out, term_gain)


def section_order(rows):
    y_size, x_size, core_size = lax.axis_size("y"), lax.axis_size("x"), lax.axis_size("core")
    shape = rows.shape
    split = rows.reshape((y_size, x_size * core_size, -1) + shape[1:])
    return jnp.swapaxes(split, 0, 1).reshape(shape)


def exchange_sum(block, axis):
    count = lax.axis_size(axis)
    pieces = block.reshape((count, block.shape[0] // count) + block.shape[1:])
    return wide_sum(lax.all_to_all(pieces.astype(jnp.bfloat16), axis, 0, 0, tiled=False))


def wide_sum(pieces):
    return jnp.sum(pieces.astype(jnp.float32), axis=0)


def reduce_terms(term_qkv, term_out, term_gain):
    rows, model_width = term_out.shape
    gain_block = jnp.zeros((rows, 128), jnp.float32).at[:, 0].set(term_gain)
    joined = section_order(jnp.concatenate([term_qkv, term_out, gain_block], axis=1))
    for axis in (("x", "core"), "y"):
        joined = exchange_sum(joined, axis)
    node_count = lax.axis_size("node")
    qkv_width = term_qkv.shape[1]
    own_rows = joined.shape[0]
    qkv_blocks = jnp.moveaxis(joined[:, :qkv_width].reshape(own_rows, node_count, -1), 1, 0)
    shared = jnp.broadcast_to(joined[None, :, qkv_width:], (node_count, own_rows, joined.shape[1] - qkv_width))
    mixed = jnp.concatenate([qkv_blocks, shared], axis=2)
    summed = wide_sum(lax.all_to_all(mixed.astype(jnp.bfloat16), "node", 0, 0, tiled=False))
    block_width = qkv_width // node_count
    part_qkv = summed[:, :block_width]
    part_out = summed[:, block_width : block_width + model_width]
    part_gain = summed[:, block_width + model_width]
    return (part_qkv, part_out, part_gain)


def solution(mesh):
    node_size, section_size = mesh.devices.shape
    core_size = 2
    x_size = 4
    y_size = section_size // (core_size * x_size)
    fine = Mesh(mesh.devices.reshape(node_size, y_size, x_size, core_size), ("node", "y", "x", "core"))
    section = ("y", "x", "core")
    return jax.shard_map(
        on_device,
        mesh=fine,
        in_specs=(P(section, "node", None), P(section, "node", None), P(), P(), P(), P(), P()),
        out_specs=(
            P(section, "node", None),
            P(section, "node", None),
            P(section, "node"),
            P(section, None),
            P(section),
        ),
        check_vma=False,
    )
```

```python
import jax
import jax.numpy as jnp
from jax import lax
from jax.experimental import pallas as pl
from jax.sharding import Mesh, PartitionSpec as P

HEADS = 4
TILE = 128


EPS = 1e-06
MASKED = -1000000000.0


def extended(block, sides, width):
    for axis, dim in sides:
        count = lax.axis_size(axis)
        forward = [(i, i + 1) for i in range(count - 1)]
        forward.append((count - 1, 0))
        backward = [(target, source) for source, target in forward]
        low = lax.ppermute(
            lax.slice_in_dim(block, block.shape[dim] - width, None, axis=dim), axis, forward
        )
        high = lax.ppermute(lax.slice_in_dim(block, 0, width, axis=dim), axis, backward)
        block = jnp.concatenate([low, block, high], axis=dim)
    return block


def passed_along(block, axis, distance):
    devices = range(lax.axis_size(axis))
    route = [((i - distance) % len(devices), i) for i in devices]
    return lax.ppermute(block, axis, route)


def tile_mask(own_lists, own_counts, first_tile, tile_total):
    tile_count = own_lists.shape[0]
    span_tiles = 3 * tile_count
    places = jnp.mod(own_lists - first_tile, tile_total)
    live_entries = jnp.arange(own_lists.shape[1], dtype=jnp.int32)[None, :] < own_counts[:, None]
    window_slots = jnp.arange(span_tiles, dtype=jnp.int32)
    matches = jnp.logical_and(
        places[:, :, None] == window_slots[None, None, :], live_entries[:, :, None]
    )
    return jnp.any(matches, axis=1)


def attention_kernel(mask_ref, q_ref, k_ref, v_ref, ga_ref, att_ref, gq_ref, gk_ref, gv_ref):
    head_dim = q_ref.shape[1]
    score_scale = head_dim ** (-0.5)
    keys = k_ref[...]
    values = v_ref[...]
    nt = (((1,), (1,)), ((), ()))
    tn = (((0,), (0,)), ((), ()))
    grad_keys = jnp.zeros(gk_ref.shape, jnp.float32)
    grad_values = jnp.zeros(gv_ref.shape, jnp.float32)
    for tile in range(q_ref.shape[0] // TILE):
        rows = slice(tile * TILE, (tile + 1) * TILE)
        queries = q_ref[rows, :]
        grads = ga_ref[rows, :]
        keep = mask_ref[tile : tile + 1, :] > 0.5
        scores = lax.dot_general(queries, keys, nt, preferred_element_type=jnp.float32) * score_scale
        scores = jnp.where(keep, scores, MASKED)
        peak = jnp.max(scores, axis=1, keepdims=True)
        expanded = jnp.exp(scores - peak)
        probabilities = expanded / jnp.sum(expanded, axis=1, keepdims=True)
        rounded = probabilities.astype(jnp.bfloat16)
        att_ref[rows, :] = jnp.dot(rounded, values, preferred_element_type=jnp.float32).astype(att_ref.dtype)
        grad_probs = lax.dot_general(grads, values, nt, preferred_element_type=jnp.float32)
        centre = jnp.sum(grad_probs * probabilities, axis=1, keepdims=True)
        grad_scores = (probabilities * (grad_probs - centre) * score_scale).astype(jnp.bfloat16)
        gq_ref[rows, :] = jnp.dot(grad_scores, keys, preferred_element_type=jnp.float32)
        grad_keys = grad_keys + lax.dot_general(grad_scores, queries, tn, preferred_element_type=jnp.float32)
        grad_values = grad_values + lax.dot_general(rounded, grads, tn, preferred_element_type=jnp.float32)
    gk_ref[...] = grad_keys
    gv_ref[...] = grad_values


def fused_attention(keep_rows, queries, window_keys, window_values, grad_attended, heads):
    rows, width = queries.shape
    span = window_keys.shape[0]
    head_dim = width // heads
    q_spec = pl.BlockSpec((rows, head_dim), lambda h: (0, h))
    w_spec = pl.BlockSpec((span, head_dim), lambda h: (0, h))
    m_spec = pl.BlockSpec(keep_rows.shape, lambda h: (0, 0))
    flops = 12 * rows * span * width
    cost = pl.CostEstimate(flops=flops, transcendentals=rows * span * heads,
                           bytes_accessed=2 * (2 * rows * width + 2 * span * width) + 4 * (rows * width + 2 * span * width) + 2 * rows * width)
    return pl.pallas_call(
        attention_kernel,
        grid=(heads,),
        in_specs=[m_spec, q_spec, w_spec, w_spec, q_spec],
        out_specs=[q_spec, q_spec, w_spec, w_spec],
        out_shape=[
            jax.ShapeDtypeStruct((rows, width), jnp.bfloat16),
            jax.ShapeDtypeStruct((rows, width), jnp.float32),
            jax.ShapeDtypeStruct((span, width), jnp.float32),
            jax.ShapeDtypeStruct((span, width), jnp.float32),
        ],
        cost_estimate=cost,
    )(keep_rows, queries, window_keys, window_values, grad_attended)


def device_step(tokens, cotangent, w_qkv, w_out, norm_gain, tile_lists, tile_counts):
    own_tokens = tokens[0]
    own_grads = cotangent[0]
    row_count, model_width = own_tokens.shape
    tile_count = row_count // TILE
    tile_total = tile_lists.shape[0]
    device = lax.axis_index("node")
    own_lists = lax.dynamic_slice_in_dim(tile_lists, device * tile_count, tile_count, 0)
    own_counts = lax.dynamic_slice_in_dim(tile_counts, device * tile_count, tile_count, 0)
    allowed = tile_mask(own_lists, own_counts, (device - 1) * tile_count, tile_total)
    widened = own_tokens.astype(jnp.float32)
    inverse_rms = lax.rsqrt(jnp.mean(widened * widened, axis=-1, keepdims=True) + EPS)
    unit_rows = widened * inverse_rms
    normed = (unit_rows * norm_gain).astype(jnp.bfloat16)
    projected = jnp.dot(normed, w_qkv, preferred_element_type=jnp.float32).astype(jnp.bfloat16)
    queries = projected[:, :model_width]
    window = extended(projected[:, model_width:], (("node", 0),), row_count)
    window_keys = window[:, :model_width]
    window_values = window[:, model_width:]
    contract_rows = (((0,), (0,)), ((), ()))
    contract_cols = (((1,), (1,)), ((), ()))
    grad_attended = lax.dot_general(
        own_grads, w_out, contract_cols, preferred_element_type=jnp.float32
    ).astype(jnp.bfloat16)
    keep_rows = jnp.zeros((8, window_keys.shape[0]), jnp.float32)
    keep_rows = keep_rows.at[:tile_count].set(jnp.repeat(allowed, TILE, axis=1).astype(jnp.float32))
    attended, grad_queries, grad_keys, grad_values = fused_attention(
        keep_rows, queries, window_keys, window_values, grad_attended, HEADS
    )
    grad_window = jnp.concatenate([grad_keys, grad_values], axis=1)
    outputs = (widened + jnp.dot(attended, w_out, preferred_element_type=jnp.float32)).astype(
        jnp.bfloat16
    )
    term_out = lax.dot_general(
        attended, own_grads, contract_rows, preferred_element_type=jnp.float32
    )
    grad_q = grad_queries.astype(jnp.bfloat16)
    term_q = lax.dot_general(normed, grad_q, contract_rows, preferred_element_type=jnp.float32)
    early = chip_ring_sum(jnp.concatenate([term_q, term_out], axis=1))
    grad_keyvals = grad_window[row_count : 2 * row_count]
    for offset, side_index in ((-1, 0), (1, 2)):
        side_part = grad_window[side_index * row_count : (side_index + 1) * row_count]
        arrived = passed_along(side_part.astype(jnp.bfloat16), "node", offset)
        grad_keyvals = grad_keyvals + arrived.astype(side_part.dtype)
    grad_kv = grad_keyvals.astype(jnp.bfloat16)
    term_kv = lax.dot_general(normed, grad_kv, contract_rows, preferred_element_type=jnp.float32)
    grad_normed = lax.dot_general(
        grad_q, w_qkv[:, :model_width], contract_cols, preferred_element_type=jnp.float32
    ) + lax.dot_general(
        grad_kv, w_qkv[:, model_width:], contract_cols, preferred_element_type=jnp.float32
    )
    term_gain = jnp.sum(grad_normed * unit_rows, axis=0)
    grad_unit = grad_normed * norm_gain
    inner_mean = jnp.mean(grad_unit * unit_rows, axis=-1, keepdims=True)
    grad_tokens = (
        own_grads.astype(jnp.float32) + inverse_rms * (grad_unit - unit_rows * inner_mean)
    ).astype(jnp.bfloat16)
    gain_block = jnp.zeros((model_width, 128), jnp.float32).at[:, 0].set(term_gain)
    late = chip_ring_sum(jnp.concatenate([term_kv, gain_block], axis=1))
    return (outputs[None], grad_tokens[None]) + node_sum(early, late, model_width)


def section_order(rows):
    y_size, x_size, core_size = lax.axis_size("y"), lax.axis_size("x"), lax.axis_size("core")
    shape = rows.shape
    split = rows.reshape((y_size, x_size, core_size, -1) + shape[1:])
    return jnp.moveaxis(split, (2, 1, 0), (0, 1, 2)).reshape(shape)


def exchange_sum(block, axis):
    count = lax.axis_size(axis)
    pieces = block.reshape((count, block.shape[0] // count) + block.shape[1:])
    return wide_sum(lax.all_to_all(pieces.astype(jnp.bfloat16), axis, 0, 0, tiled=False))


def wide_sum(pieces):
    return jnp.sum(pieces.astype(jnp.float32), axis=0)


def node_sum(early, late, model_width):
    joined = jnp.concatenate([early, late], axis=1)
    joined = exchange_sum(joined, "y")
    early, late = joined[:, : 2 * model_width], joined[:, 2 * model_width :]
    node_count = lax.axis_size("node")
    own_rows = early.shape[0]
    qkv = jnp.concatenate([early[:, :model_width], late[:, : 2 * model_width]], axis=1)
    rest = jnp.concatenate([early[:, model_width:], late[:, 2 * model_width :]], axis=1)
    qkv_blocks = jnp.moveaxis(qkv.reshape(own_rows, node_count, -1), 1, 0)
    shared = jnp.broadcast_to(rest[None], (node_count,) + rest.shape)
    mixed = jnp.concatenate([qkv_blocks, shared], axis=2)
    summed = wide_sum(lax.all_to_all(mixed.astype(jnp.bfloat16), "node", 0, 0, tiled=False))
    block_width = qkv.shape[1] // node_count
    part_qkv = summed[:, :block_width]
    part_out = summed[:, block_width : block_width + model_width]
    part_gain = summed[:, block_width + model_width]
    return (part_qkv, part_out, part_gain)


def chip_ring_sum(term):
    joined = section_order(term)
    for axis in ("core", "x"):
        joined = exchange_sum(joined, axis)
    return joined


def solution(mesh):
    node_size, section_size = mesh.devices.shape
    core_size = 2
    x_size = 4
    y_size = section_size // (core_size * x_size)
    fine = Mesh(mesh.devices.reshape(node_size, y_size, x_size, core_size), ("node", "y", "x", "core"))
    section = ("y", "x", "core")
    return jax.shard_map(
        device_step,
        mesh=fine,
        in_specs=(P(section, "node", None), P(section, "node", None), P(), P(), P(), P(), P()),
        out_specs=(
            P(section, "node", None),
            P(section, "node", None),
            P(section, "node"),
            P(section, None),
            P(section),
        ),
        check_vma=False,
    )
```

```python
import jax
import jax.numpy as jnp
from jax import lax
from jax.experimental import pallas as pl
from jax.sharding import Mesh, PartitionSpec as P

HEADS = 4
TILE = 128


EPS = 1e-06
MASKED = -1000000000.0


def extended(block, sides, width):
    for axis, dim in sides:
        count = lax.axis_size(axis)
        forward = [(i, i + 1) for i in range(count - 1)]
        forward.append((count - 1, 0))
        backward = [(target, source) for source, target in forward]
        low = lax.ppermute(
            lax.slice_in_dim(block, block.shape[dim] - width, None, axis=dim), axis, forward
        )
        high = lax.ppermute(lax.slice_in_dim(block, 0, width, axis=dim), axis, backward)
        block = jnp.concatenate([low, block, high], axis=dim)
    return block


def passed_along(block, axis, distance):
    devices = range(lax.axis_size(axis))
    route = [((i - distance) % len(devices), i) for i in devices]
    return lax.ppermute(block, axis, route)


def tile_mask(own_lists, own_counts, first_tile, tile_total):
    tile_count = own_lists.shape[0]
    span_tiles = 3 * tile_count
    places = jnp.mod(own_lists - first_tile, tile_total)
    live_entries = jnp.arange(own_lists.shape[1], dtype=jnp.int32)[None, :] < own_counts[:, None]
    window_slots = jnp.arange(span_tiles, dtype=jnp.int32)
    matches = jnp.logical_and(
        places[:, :, None] == window_slots[None, None, :], live_entries[:, :, None]
    )
    return jnp.any(matches, axis=1)


def attention_kernel(mask_ref, q_ref, k_ref, v_ref, ga_ref, att_ref, gq_ref, gk_ref, gv_ref):
    head_dim = q_ref.shape[1]
    score_scale = head_dim ** (-0.5)
    keys = k_ref[...]
    values = v_ref[...]
    nt = (((1,), (1,)), ((), ()))
    tn = (((0,), (0,)), ((), ()))
    grad_keys = jnp.zeros(gk_ref.shape, jnp.float32)
    grad_values = jnp.zeros(gv_ref.shape, jnp.float32)
    for tile in range(q_ref.shape[0] // TILE):
        rows = slice(tile * TILE, (tile + 1) * TILE)
        queries = q_ref[rows, :]
        grads = ga_ref[rows, :]
        keep = mask_ref[tile : tile + 1, :] > 0.5
        scores = lax.dot_general(queries, keys, nt, preferred_element_type=jnp.float32) * score_scale
        scores = jnp.where(keep, scores, MASKED)
        peak = jnp.max(scores, axis=1, keepdims=True)
        expanded = jnp.exp(scores - peak)
        probabilities = expanded / jnp.sum(expanded, axis=1, keepdims=True)
        rounded = probabilities.astype(jnp.bfloat16)
        att_ref[rows, :] = jnp.dot(rounded, values, preferred_element_type=jnp.float32).astype(att_ref.dtype)
        grad_probs = lax.dot_general(grads, values, nt, preferred_element_type=jnp.float32)
        centre = jnp.sum(grad_probs * probabilities, axis=1, keepdims=True)
        grad_scores = (probabilities * (grad_probs - centre) * score_scale).astype(jnp.bfloat16)
        gq_ref[rows, :] = jnp.dot(grad_scores, keys, preferred_element_type=jnp.float32)
        grad_keys = grad_keys + lax.dot_general(grad_scores, queries, tn, preferred_element_type=jnp.float32)
        grad_values = grad_values + lax.dot_general(rounded, grads, tn, preferred_element_type=jnp.float32)
    gk_ref[...] = grad_keys
    gv_ref[...] = grad_values


def fused_attention(keep_rows, queries, window_keys, window_values, grad_attended, heads):
    rows, width = queries.shape
    span = window_keys.shape[0]
    head_dim = width // heads
    q_spec = pl.BlockSpec((rows, head_dim), lambda h: (0, h))
    w_spec = pl.BlockSpec((span, head_dim), lambda h: (0, h))
    m_spec = pl.BlockSpec(keep_rows.shape, lambda h: (0, 0))
    flops = 12 * rows * span * width
    cost = pl.CostEstimate(flops=flops, transcendentals=rows * span * heads,
                           bytes_accessed=2 * (2 * rows * width + 2 * span * width) + 4 * (rows * width + 2 * span * width) + 2 * rows * width)
    return pl.pallas_call(
        attention_kernel,
        grid=(heads,),
        in_specs=[m_spec, q_spec, w_spec, w_spec, q_spec],
        out_specs=[q_spec, q_spec, w_spec, w_spec],
        out_shape=[
            jax.ShapeDtypeStruct((rows, width), jnp.bfloat16),
            jax.ShapeDtypeStruct((rows, width), jnp.float32),
            jax.ShapeDtypeStruct((span, width), jnp.float32),
            jax.ShapeDtypeStruct((span, width), jnp.float32),
        ],
        cost_estimate=cost,
    )(keep_rows, queries, window_keys, window_values, grad_attended)


def device_step(tokens, cotangent, w_qkv, w_out, norm_gain, tile_lists, tile_counts):
    own_tokens = tokens[0]
    own_grads = cotangent[0]
    row_count, model_width = own_tokens.shape
    tile_count = row_count // TILE
    tile_total = tile_lists.shape[0]
    device = lax.axis_index("node")
    own_lists = lax.dynamic_slice_in_dim(tile_lists, device * tile_count, tile_count, 0)
    own_counts = lax.dynamic_slice_in_dim(tile_counts, device * tile_count, tile_count, 0)
    allowed = tile_mask(own_lists, own_counts, (device - 1) * tile_count, tile_total)
    widened = own_tokens.astype(jnp.float32)
    inverse_rms = lax.rsqrt(jnp.mean(widened * widened, axis=-1, keepdims=True) + EPS)
    unit_rows = widened * inverse_rms
    normed = (unit_rows * norm_gain).astype(jnp.bfloat16)
    projected = jnp.dot(normed, w_qkv, preferred_element_type=jnp.float32).astype(jnp.bfloat16)
    queries = projected[:, :model_width]
    window = extended(projected[:, model_width:], (("node", 0),), row_count)
    window_keys = window[:, :model_width]
    window_values = window[:, model_width:]
    contract_rows = (((0,), (0,)), ((), ()))
    contract_cols = (((1,), (1,)), ((), ()))
    grad_attended = lax.dot_general(
        own_grads, w_out, contract_cols, preferred_element_type=jnp.float32
    ).astype(jnp.bfloat16)
    keep_rows = jnp.zeros((8, window_keys.shape[0]), jnp.float32)
    keep_rows = keep_rows.at[:tile_count].set(jnp.repeat(allowed, TILE, axis=1).astype(jnp.float32))
    attended, grad_queries, grad_keys, grad_values = fused_attention(
        keep_rows, queries, window_keys, window_values, grad_attended, HEADS
    )
    grad_window = jnp.concatenate([grad_keys, grad_values], axis=1)
    outputs = (widened + jnp.dot(attended, w_out, preferred_element_type=jnp.float32)).astype(
        jnp.bfloat16
    )
    term_out = lax.dot_general(
        attended, own_grads, contract_rows, preferred_element_type=jnp.float32
    )
    grad_q = grad_queries.astype(jnp.bfloat16)
    term_q = lax.dot_general(normed, grad_q, contract_rows, preferred_element_type=jnp.float32)
    early = chip_sum(jnp.concatenate([term_q, term_out], axis=1))
    grad_keyvals = grad_window[row_count : 2 * row_count]
    for offset, side_index in ((-1, 0), (1, 2)):
        side_part = grad_window[side_index * row_count : (side_index + 1) * row_count]
        arrived = passed_along(side_part.astype(jnp.bfloat16), "node", offset)
        grad_keyvals = grad_keyvals + arrived.astype(side_part.dtype)
    grad_kv = grad_keyvals.astype(jnp.bfloat16)
    term_kv = lax.dot_general(normed, grad_kv, contract_rows, preferred_element_type=jnp.float32)
    grad_normed = lax.dot_general(
        grad_q, w_qkv[:, :model_width], contract_cols, preferred_element_type=jnp.float32
    ) + lax.dot_general(
        grad_kv, w_qkv[:, model_width:], contract_cols, preferred_element_type=jnp.float32
    )
    term_gain = jnp.sum(grad_normed * unit_rows, axis=0)
    grad_unit = grad_normed * norm_gain
    inner_mean = jnp.mean(grad_unit * unit_rows, axis=-1, keepdims=True)
    grad_tokens = (
        own_grads.astype(jnp.float32) + inverse_rms * (grad_unit - unit_rows * inner_mean)
    ).astype(jnp.bfloat16)
    gain_block = jnp.zeros((model_width, 128), jnp.float32).at[:, 0].set(term_gain)
    late = chip_sum(jnp.concatenate([term_kv, gain_block], axis=1))
    return (outputs[None], grad_tokens[None]) + node_sum(early, late, model_width)


def section_order(rows):
    y_size, x_size, core_size = lax.axis_size("y"), lax.axis_size("x"), lax.axis_size("core")
    shape = rows.shape
    split = rows.reshape((y_size, x_size, core_size, -1) + shape[1:])
    return jnp.moveaxis(split, (2, 1, 0), (0, 1, 2)).reshape(shape)


def exchange_sum(block, axis):
    count = lax.axis_size(axis)
    pieces = block.reshape((count, block.shape[0] // count) + block.shape[1:])
    return wide_sum(lax.all_to_all(pieces.astype(jnp.bfloat16), axis, 0, 0, tiled=False))


def wide_sum(pieces):
    return jnp.sum(pieces.astype(jnp.float32), axis=0)


def node_sum(early, late, model_width):
    joined = jnp.concatenate([early, late], axis=1)
    for axis in ("x", "y"):
        joined = exchange_sum(joined, axis)
    early, late = joined[:, : 2 * model_width], joined[:, 2 * model_width :]
    node_count = lax.axis_size("node")
    own_rows = early.shape[0]
    qkv = jnp.concatenate([early[:, :model_width], late[:, : 2 * model_width]], axis=1)
    rest = jnp.concatenate([early[:, model_width:], late[:, 2 * model_width :]], axis=1)
    qkv_blocks = jnp.moveaxis(qkv.reshape(own_rows, node_count, -1), 1, 0)
    shared = jnp.broadcast_to(rest[None], (node_count,) + rest.shape)
    mixed = jnp.concatenate([qkv_blocks, shared], axis=2)
    summed = wide_sum(lax.all_to_all(mixed.astype(jnp.bfloat16), "node", 0, 0, tiled=False))
    block_width = qkv.shape[1] // node_count
    part_qkv = summed[:, :block_width]
    part_out = summed[:, block_width : block_width + model_width]
    part_gain = summed[:, block_width + model_width]
    return (part_qkv, part_out, part_gain)


def chip_sum(term):
    return exchange_sum(section_order(term), "core")


def solution(mesh):
    node_size, section_size = mesh.devices.shape
    core_size = 2
    x_size = 4
    y_size = section_size // (core_size * x_size)
    fine = Mesh(mesh.devices.reshape(node_size, y_size, x_size, core_size), ("node", "y", "x", "core"))
    section = ("y", "x", "core")
    return jax.shard_map(
        device_step,
        mesh=fine,
        in_specs=(P(section, "node", None), P(section, "node", None), P(), P(), P(), P(), P()),
        out_specs=(
            P(section, "node", None),
            P(section, "node", None),
            P(section, "node"),
            P(section, None),
            P(section),
        ),
        check_vma=False,
    )
```

```python
import jax
import jax.numpy as jnp
from jax import lax
from jax.experimental import pallas as pl
from jax.sharding import Mesh, PartitionSpec as P

HEADS = 4
TILE = 128


EPS = 1e-06
MASKED = -1000000000.0


def passed_along(block, axis, distance):
    devices = range(lax.axis_size(axis))
    route = [((i - distance) % len(devices), i) for i in devices]
    return lax.ppermute(block, axis, route)


def tile_mask(own_lists, own_counts, first_tile, tile_total):
    tile_count = own_lists.shape[0]
    span_tiles = 3 * tile_count
    places = jnp.mod(own_lists - first_tile, tile_total)
    live_entries = jnp.arange(own_lists.shape[1], dtype=jnp.int32)[None, :] < own_counts[:, None]
    window_slots = jnp.arange(span_tiles, dtype=jnp.int32)
    matches = jnp.logical_and(
        places[:, :, None] == window_slots[None, None, :], live_entries[:, :, None]
    )
    return jnp.any(matches, axis=1)


def attention_kernel(mask_ref, q_ref, k_ref, v_ref, kp_ref, vp_ref, kn_ref, vn_ref, ga_ref,
                     att_ref, gq_ref, gk_ref, gv_ref, gkp_ref, gvp_ref, gkn_ref, gvn_ref):
    head_dim = q_ref.shape[1]
    block_rows = k_ref.shape[0]
    score_scale = head_dim ** (-0.5)
    keys = jnp.concatenate([kp_ref[...], k_ref[...], kn_ref[...]], axis=0)
    values = jnp.concatenate([vp_ref[...], v_ref[...], vn_ref[...]], axis=0)
    nt = (((1,), (1,)), ((), ()))
    tn = (((0,), (0,)), ((), ()))
    grad_keys = jnp.zeros(keys.shape, jnp.float32)
    grad_values = jnp.zeros(values.shape, jnp.float32)
    for tile in range(q_ref.shape[0] // TILE):
        rows = slice(tile * TILE, (tile + 1) * TILE)
        queries = q_ref[rows, :]
        grads = ga_ref[rows, :]
        keep = mask_ref[tile : tile + 1, :] > 0.5
        scores = lax.dot_general(queries, keys, nt, preferred_element_type=jnp.float32) * score_scale
        scores = jnp.where(keep, scores, MASKED)
        peak = jnp.max(scores, axis=1, keepdims=True)
        expanded = jnp.exp(scores - peak)
        probabilities = expanded / jnp.sum(expanded, axis=1, keepdims=True)
        rounded = probabilities.astype(jnp.bfloat16)
        att_ref[rows, :] = jnp.dot(rounded, values, preferred_element_type=jnp.float32).astype(att_ref.dtype)
        grad_probs = lax.dot_general(grads, values, nt, preferred_element_type=jnp.float32)
        centre = jnp.sum(grad_probs * probabilities, axis=1, keepdims=True)
        grad_scores = (probabilities * (grad_probs - centre) * score_scale).astype(jnp.bfloat16)
        gq_ref[rows, :] = jnp.dot(grad_scores, keys, preferred_element_type=jnp.float32).astype(gq_ref.dtype)
        grad_keys = grad_keys + lax.dot_general(grad_scores, queries, tn, preferred_element_type=jnp.float32)
        grad_values = grad_values + lax.dot_general(rounded, grads, tn, preferred_element_type=jnp.float32)
    gkp_ref[...] = grad_keys[:block_rows].astype(gkp_ref.dtype)
    gvp_ref[...] = grad_values[:block_rows].astype(gvp_ref.dtype)
    gk_ref[...] = grad_keys[block_rows : 2 * block_rows]
    gv_ref[...] = grad_values[block_rows : 2 * block_rows]
    gkn_ref[...] = grad_keys[2 * block_rows :].astype(gkn_ref.dtype)
    gvn_ref[...] = grad_values[2 * block_rows :].astype(gvn_ref.dtype)


def fused_attention(keep_rows, projected, low, high, grad_attended, heads):
    rows, width = grad_attended.shape
    head_dim = width // heads
    span = 3 * rows

    def column(offset):
        return pl.BlockSpec((rows, head_dim), lambda h: (0, h + offset))

    m_spec = pl.BlockSpec(keep_rows.shape, lambda h: (0, 0))
    cost = pl.CostEstimate(flops=12 * rows * span * width, transcendentals=rows * span * heads,
                           bytes_accessed=2 * (3 * rows * width + 2 * span * width) + 4 * (2 * rows * width) + 2 * (5 * rows * width))
    bf16_out = jax.ShapeDtypeStruct((rows, width), jnp.bfloat16)
    f32_out = jax.ShapeDtypeStruct((rows, width), jnp.float32)
    return pl.pallas_call(
        attention_kernel,
        grid=(heads,),
        in_specs=[m_spec, column(0), column(heads), column(2 * heads), column(0), column(heads),
                  column(0), column(heads), column(0)],
        out_specs=[column(0)] * 8,
        out_shape=[bf16_out, bf16_out, f32_out, f32_out, bf16_out, bf16_out, bf16_out, bf16_out],
        cost_estimate=cost,
    )(keep_rows, projected, projected, projected, low, low, high, high, grad_attended)


def device_step(tokens, cotangent, w_qkv, w_out, norm_gain, tile_lists, tile_counts):
    own_tokens = tokens[0]
    own_grads = cotangent[0]
    row_count, model_width = own_tokens.shape
    tile_count = row_count // TILE
    tile_total = tile_lists.shape[0]
    device = lax.axis_index("node")
    own_lists = lax.dynamic_slice_in_dim(tile_lists, device * tile_count, tile_count, 0)
    own_counts = lax.dynamic_slice_in_dim(tile_counts, device * tile_count, tile_count, 0)
    allowed = tile_mask(own_lists, own_counts, (device - 1) * tile_count, tile_total)
    widened = own_tokens.astype(jnp.float32)
    inverse_rms = lax.rsqrt(jnp.mean(widened * widened, axis=-1, keepdims=True) + EPS)
    unit_rows = widened * inverse_rms
    normed = (unit_rows * norm_gain).astype(jnp.bfloat16)
    projected = jnp.dot(normed, w_qkv, preferred_element_type=jnp.float32).astype(jnp.bfloat16)
    keyvals = projected[:, model_width:]
    low = passed_along(keyvals, "node", 1)
    high = passed_along(keyvals, "node", -1)
    contract_rows = (((0,), (0,)), ((), ()))
    contract_cols = (((1,), (1,)), ((), ()))
    grad_attended = lax.dot_general(
        own_grads, w_out, contract_cols, preferred_element_type=jnp.float32
    ).astype(jnp.bfloat16)
    keep_rows = jnp.zeros((8, 3 * row_count), jnp.float32)
    keep_rows = keep_rows.at[:tile_count].set(jnp.repeat(allowed, TILE, axis=1).astype(jnp.float32))
    (attended, grad_q, grad_keys, grad_values, low_keys, low_values, high_keys, high_values) = (
        fused_attention(keep_rows, projected, low, high, grad_attended, HEADS)
    )
    outputs = (widened + jnp.dot(attended, w_out, preferred_element_type=jnp.float32)).astype(
        jnp.bfloat16
    )
    term_out = lax.dot_general(
        attended, own_grads, contract_rows, preferred_element_type=jnp.float32
    )
    term_q = lax.dot_general(normed, grad_q, contract_rows, preferred_element_type=jnp.float32)
    early = chip_sum(jnp.concatenate([term_q, term_out], axis=1))
    grad_keyvals = jnp.concatenate([grad_keys, grad_values], axis=1)
    for offset, side_keys, side_values in ((-1, low_keys, low_values), (1, high_keys, high_values)):
        side_part = jnp.concatenate([side_keys, side_values], axis=1)
        arrived = passed_along(side_part, "node", offset)
        grad_keyvals = grad_keyvals + arrived.astype(jnp.float32)
    grad_kv = grad_keyvals.astype(jnp.bfloat16)
    term_kv = lax.dot_general(normed, grad_kv, contract_rows, preferred_element_type=jnp.float32)
    grad_normed = lax.dot_general(
        grad_q, w_qkv[:, :model_width], contract_cols, preferred_element_type=jnp.float32
    ) + lax.dot_general(
        grad_kv, w_qkv[:, model_width:], contract_cols, preferred_element_type=jnp.float32
    )
    term_gain = jnp.sum(grad_normed * unit_rows, axis=0)
    grad_unit = grad_normed * norm_gain
    inner_mean = jnp.mean(grad_unit * unit_rows, axis=-1, keepdims=True)
    grad_tokens = (
        own_grads.astype(jnp.float32) + inverse_rms * (grad_unit - unit_rows * inner_mean)
    ).astype(jnp.bfloat16)
    gain_block = jnp.zeros((model_width, 128), jnp.float32).at[:, 0].set(term_gain)
    late = chip_sum(jnp.concatenate([term_kv, gain_block], axis=1))
    return (outputs[None], grad_tokens[None]) + node_sum(early, late, model_width)


def section_order(rows):
    y_size, x_size, core_size = lax.axis_size("y"), lax.axis_size("x"), lax.axis_size("core")
    shape = rows.shape
    split = rows.reshape((y_size, x_size, core_size, -1) + shape[1:])
    return jnp.moveaxis(split, (2, 1, 0), (0, 1, 2)).reshape(shape)


def exchange_sum(block, axis):
    count = lax.axis_size(axis)
    pieces = block.reshape((count, block.shape[0] // count) + block.shape[1:])
    return wide_sum(lax.all_to_all(pieces.astype(jnp.bfloat16), axis, 0, 0, tiled=False))


def wide_sum(pieces):
    return jnp.sum(pieces.astype(jnp.float32), axis=0)


def node_sum(early, late, model_width):
    joined = jnp.concatenate([early, late], axis=1)
    for axis in ("x", "y"):
        joined = exchange_sum(joined, axis)
    early, late = joined[:, : 2 * model_width], joined[:, 2 * model_width :]
    node_count = lax.axis_size("node")
    own_rows = early.shape[0]
    qkv = jnp.concatenate([early[:, :model_width], late[:, : 2 * model_width]], axis=1)
    rest = jnp.concatenate([early[:, model_width:], late[:, 2 * model_width :]], axis=1)
    qkv_blocks = jnp.moveaxis(qkv.reshape(own_rows, node_count, -1), 1, 0)
    shared = jnp.broadcast_to(rest[None], (node_count,) + rest.shape)
    mixed = jnp.concatenate([qkv_blocks, shared], axis=2)
    summed = wide_sum(lax.all_to_all(mixed.astype(jnp.bfloat16), "node", 0, 0, tiled=False))
    block_width = qkv.shape[1] // node_count
    part_qkv = summed[:, :block_width]
    part_out = summed[:, block_width : block_width + model_width]
    part_gain = summed[:, block_width + model_width]
    return (part_qkv, part_out, part_gain)


def chip_sum(term):
    return exchange_sum(section_order(term), "core")


def solution(mesh):
    node_size, section_size = mesh.devices.shape
    core_size = 2
    x_size = 4
    y_size = section_size // (core_size * x_size)
    fine = Mesh(mesh.devices.reshape(node_size, y_size, x_size, core_size), ("node", "y", "x", "core"))
    section = ("y", "x", "core")
    return jax.shard_map(
        device_step,
        mesh=fine,
        in_specs=(P(section, "node", None), P(section, "node", None), P(), P(), P(), P(), P()),
        out_specs=(
            P(section, "node", None),
            P(section, "node", None),
            P(section, "node"),
            P(section, None),
            P(section),
        ),
        check_vma=False,
    )
```

```python
import jax
import jax.numpy as jnp
from jax import lax
from jax.experimental import pallas as pl
from jax.sharding import Mesh, PartitionSpec as P

HEADS = 4
TILE = 128


EPS = 1e-06
MASKED = -1000000000.0


def passed_along(block, axis, distance):
    devices = range(lax.axis_size(axis))
    route = [((i - distance) % len(devices), i) for i in devices]
    return lax.ppermute(block, axis, route)


def tile_mask(own_lists, own_counts, first_tile, tile_total):
    tile_count = own_lists.shape[0]
    span_tiles = 3 * tile_count
    places = jnp.mod(own_lists - first_tile, tile_total)
    live_entries = jnp.arange(own_lists.shape[1], dtype=jnp.int32)[None, :] < own_counts[:, None]
    window_slots = jnp.arange(span_tiles, dtype=jnp.int32)
    matches = jnp.logical_and(
        places[:, :, None] == window_slots[None, None, :], live_entries[:, :, None]
    )
    return jnp.any(matches, axis=1)


def attention_kernel(mask_ref, q_ref, k_ref, v_ref, kp_ref, vp_ref, kn_ref, vn_ref, ga_ref,
                     att_ref, gq_ref, own_ref, low_ref, high_ref):
    head_dim = q_ref.shape[1]
    block_rows = k_ref.shape[0]
    score_scale = head_dim ** (-0.5)
    keys = jnp.concatenate([kp_ref[...], k_ref[...], kn_ref[...]], axis=0)
    values = jnp.concatenate([vp_ref[...], v_ref[...], vn_ref[...]], axis=0)
    nt = (((1,), (1,)), ((), ()))
    tn = (((0,), (0,)), ((), ()))
    grad_keys = jnp.zeros(keys.shape, jnp.float32)
    grad_values = jnp.zeros(values.shape, jnp.float32)
    for tile in range(q_ref.shape[0] // TILE):
        rows = slice(tile * TILE, (tile + 1) * TILE)
        queries = q_ref[rows, :]
        grads = ga_ref[rows, :]
        keep = mask_ref[tile : tile + 1, :] > 0.5
        scores = lax.dot_general(queries, keys, nt, preferred_element_type=jnp.float32) * score_scale
        scores = jnp.where(keep, scores, MASKED)
        peak = jnp.max(scores, axis=1, keepdims=True)
        expanded = jnp.exp(scores - peak)
        probabilities = expanded / jnp.sum(expanded, axis=1, keepdims=True)
        rounded = probabilities.astype(jnp.bfloat16)
        att_ref[rows, :] = jnp.dot(rounded, values, preferred_element_type=jnp.float32).astype(att_ref.dtype)
        grad_probs = lax.dot_general(grads, values, nt, preferred_element_type=jnp.float32)
        centre = jnp.sum(grad_probs * probabilities, axis=1, keepdims=True)
        grad_scores = (probabilities * (grad_probs - centre) * score_scale).astype(jnp.bfloat16)
        gq_ref[rows, :] = jnp.dot(grad_scores, keys, preferred_element_type=jnp.float32).astype(gq_ref.dtype)
        grad_keys = grad_keys + lax.dot_general(grad_scores, queries, tn, preferred_element_type=jnp.float32)
        grad_values = grad_values + lax.dot_general(rounded, grads, tn, preferred_element_type=jnp.float32)
    for side, side_ref in enumerate((low_ref, own_ref, high_ref)):
        part = slice(side * block_rows, (side + 1) * block_rows)
        side_ref[0] = grad_keys[part].astype(side_ref.dtype)
        side_ref[1] = grad_values[part].astype(side_ref.dtype)


def fused_attention(keep_rows, projected, low, high, grad_attended, heads):
    rows, width = grad_attended.shape
    head_dim = width // heads
    span = 3 * rows

    def column(offset):
        return pl.BlockSpec((rows, head_dim), lambda h: (0, h + offset))

    m_spec = pl.BlockSpec(keep_rows.shape, lambda h: (0, 0))
    cost = pl.CostEstimate(flops=12 * rows * span * width, transcendentals=rows * span * heads,
                           bytes_accessed=2 * (3 * rows * width + 2 * span * width) + 4 * (2 * rows * width) + 2 * (5 * rows * width))
    bf16_out = jax.ShapeDtypeStruct((rows, width), jnp.bfloat16)
    pair_spec = pl.BlockSpec((2, rows, head_dim), lambda h: (0, 0, h))
    return pl.pallas_call(
        attention_kernel,
        grid=(heads,),
        in_specs=[m_spec, column(0), column(heads), column(2 * heads), column(0), column(heads),
                  column(0), column(heads), column(0)],
        out_specs=[column(0), column(0), pair_spec, pair_spec, pair_spec],
        out_shape=[
            bf16_out,
            bf16_out,
            jax.ShapeDtypeStruct((2, rows, width), jnp.float32),
            jax.ShapeDtypeStruct((2, rows, width), jnp.bfloat16),
            jax.ShapeDtypeStruct((2, rows, width), jnp.bfloat16),
        ],
        cost_estimate=cost,
    )(keep_rows, projected, projected, projected, low, low, high, high, grad_attended)


def device_step(tokens, cotangent, w_qkv, w_out, norm_gain, tile_lists, tile_counts):
    own_tokens = tokens[0]
    own_grads = cotangent[0]
    row_count, model_width = own_tokens.shape
    tile_count = row_count // TILE
    tile_total = tile_lists.shape[0]
    device = lax.axis_index("node")
    own_lists = lax.dynamic_slice_in_dim(tile_lists, device * tile_count, tile_count, 0)
    own_counts = lax.dynamic_slice_in_dim(tile_counts, device * tile_count, tile_count, 0)
    allowed = tile_mask(own_lists, own_counts, (device - 1) * tile_count, tile_total)
    widened = own_tokens.astype(jnp.float32)
    inverse_rms = lax.rsqrt(jnp.mean(widened * widened, axis=-1, keepdims=True) + EPS)
    unit_rows = widened * inverse_rms
    normed = (unit_rows * norm_gain).astype(jnp.bfloat16)
    projected = jnp.dot(normed, w_qkv, preferred_element_type=jnp.float32).astype(jnp.bfloat16)
    keyvals = projected[:, model_width:]
    low = passed_along(keyvals, "node", 1)
    high = passed_along(keyvals, "node", -1)
    contract_rows = (((0,), (0,)), ((), ()))
    contract_cols = (((1,), (1,)), ((), ()))
    grad_attended = lax.dot_general(
        own_grads, w_out, contract_cols, preferred_element_type=jnp.float32
    ).astype(jnp.bfloat16)
    keep_rows = jnp.zeros((8, 3 * row_count), jnp.float32)
    keep_rows = keep_rows.at[:tile_count].set(jnp.repeat(allowed, TILE, axis=1).astype(jnp.float32))
    attended, grad_q, grad_own, grad_low, grad_high = fused_attention(
        keep_rows, projected, low, high, grad_attended, HEADS
    )
    outputs = (widened + jnp.dot(attended, w_out, preferred_element_type=jnp.float32)).astype(
        jnp.bfloat16
    )
    term_out = lax.dot_general(
        attended, own_grads, contract_rows, preferred_element_type=jnp.float32
    )
    term_q = lax.dot_general(normed, grad_q, contract_rows, preferred_element_type=jnp.float32)
    early = chip_sum(jnp.concatenate([term_q, term_out], axis=1))
    grad_pair = grad_own
    for offset, side_part in ((-1, grad_low), (1, grad_high)):
        arrived = passed_along(side_part, "node", offset)
        grad_pair = grad_pair + arrived.astype(jnp.float32)
    grad_keyvals = jnp.concatenate([grad_pair[0], grad_pair[1]], axis=1)
    grad_kv = grad_keyvals.astype(jnp.bfloat16)
    term_kv = lax.dot_general(normed, grad_kv, contract_rows, preferred_element_type=jnp.float32)
    grad_normed = lax.dot_general(
        grad_q, w_qkv[:, :model_width], contract_cols, preferred_element_type=jnp.float32
    ) + lax.dot_general(
        grad_kv, w_qkv[:, model_width:], contract_cols, preferred_element_type=jnp.float32
    )
    term_gain = jnp.sum(grad_normed * unit_rows, axis=0)
    grad_unit = grad_normed * norm_gain
    inner_mean = jnp.mean(grad_unit * unit_rows, axis=-1, keepdims=True)
    grad_tokens = (
        own_grads.astype(jnp.float32) + inverse_rms * (grad_unit - unit_rows * inner_mean)
    ).astype(jnp.bfloat16)
    gain_block = jnp.zeros((model_width, 128), jnp.float32).at[:, 0].set(term_gain)
    late = chip_sum(jnp.concatenate([term_kv, gain_block], axis=1))
    return (outputs[None], grad_tokens[None]) + node_sum(early, late, model_width)


def section_order(rows):
    y_size, x_size, core_size = lax.axis_size("y"), lax.axis_size("x"), lax.axis_size("core")
    shape = rows.shape
    split = rows.reshape((y_size, x_size, core_size, -1) + shape[1:])
    return jnp.moveaxis(split, (2, 1, 0), (0, 1, 2)).reshape(shape)


def exchange_sum(block, axis):
    count = lax.axis_size(axis)
    pieces = block.reshape((count, block.shape[0] // count) + block.shape[1:])
    return wide_sum(lax.all_to_all(pieces.astype(jnp.bfloat16), axis, 0, 0, tiled=False))


def wide_sum(pieces):
    return jnp.sum(pieces.astype(jnp.float32), axis=0)


def node_sum(early, late, model_width):
    joined = jnp.concatenate([early, late], axis=1)
    for axis in ("x", "y"):
        joined = exchange_sum(joined, axis)
    early, late = joined[:, : 2 * model_width], joined[:, 2 * model_width :]
    node_count = lax.axis_size("node")
    own_rows = early.shape[0]
    qkv = jnp.concatenate([early[:, :model_width], late[:, : 2 * model_width]], axis=1)
    rest = jnp.concatenate([early[:, model_width:], late[:, 2 * model_width :]], axis=1)
    qkv_blocks = jnp.moveaxis(qkv.reshape(own_rows, node_count, -1), 1, 0)
    shared = jnp.broadcast_to(rest[None], (node_count,) + rest.shape)
    mixed = jnp.concatenate([qkv_blocks, shared], axis=2)
    summed = wide_sum(lax.all_to_all(mixed.astype(jnp.bfloat16), "node", 0, 0, tiled=False))
    block_width = qkv.shape[1] // node_count
    part_qkv = summed[:, :block_width]
    part_out = summed[:, block_width : block_width + model_width]
    part_gain = summed[:, block_width + model_width]
    return (part_qkv, part_out, part_gain)


def chip_sum(term):
    return exchange_sum(section_order(term), "core")


def solution(mesh):
    node_size, section_size = mesh.devices.shape
    core_size = 2
    x_size = 4
    y_size = section_size // (core_size * x_size)
    fine = Mesh(mesh.devices.reshape(node_size, y_size, x_size, core_size), ("node", "y", "x", "core"))
    section = ("y", "x", "core")
    return jax.shard_map(
        device_step,
        mesh=fine,
        in_specs=(P(section, "node", None), P(section, "node", None), P(), P(), P(), P(), P()),
        out_specs=(
            P(section, "node", None),
            P(section, "node", None),
            P(section, "node"),
            P(section, None),
            P(section),
        ),
        check_vma=False,
    )
```

```python
import jax
import jax.numpy as jnp
from jax import lax
from jax.experimental import pallas as pl
from jax.sharding import Mesh, PartitionSpec as P

HEADS = 4
TILE = 128


EPS = 1e-06
MASKED = -1000000000.0


def passed_along(block, axis, distance):
    devices = range(lax.axis_size(axis))
    route = [((i - distance) % len(devices), i) for i in devices]
    return lax.ppermute(block, axis, route)


def tile_mask(own_lists, own_counts, first_tile, tile_total):
    tile_count = own_lists.shape[0]
    span_tiles = 3 * tile_count
    places = jnp.mod(own_lists - first_tile, tile_total)
    live_entries = jnp.arange(own_lists.shape[1], dtype=jnp.int32)[None, :] < own_counts[:, None]
    window_slots = jnp.arange(span_tiles, dtype=jnp.int32)
    matches = jnp.logical_and(
        places[:, :, None] == window_slots[None, None, :], live_entries[:, :, None]
    )
    return jnp.any(matches, axis=1)


def attention_kernel(mask_ref, q_ref, k_ref, v_ref, kp_ref, vp_ref, kn_ref, vn_ref, ga_ref,
                     att_ref, gq_ref, own_ref, low_ref, high_ref):
    head_dim = q_ref.shape[1]
    block_rows = k_ref.shape[0]
    score_scale = head_dim ** (-0.5)
    keys = jnp.concatenate([kp_ref[...], k_ref[...], kn_ref[...]], axis=0)
    values = jnp.concatenate([vp_ref[...], v_ref[...], vn_ref[...]], axis=0)
    nt = (((1,), (1,)), ((), ()))
    tn = (((0,), (0,)), ((), ()))
    grad_keys = jnp.zeros(keys.shape, jnp.float32)
    grad_values = jnp.zeros(values.shape, jnp.float32)
    for tile in range(q_ref.shape[0] // TILE):
        rows = slice(tile * TILE, (tile + 1) * TILE)
        queries = q_ref[rows, :]
        grads = ga_ref[rows, :]
        keep = mask_ref[tile : tile + 1, :] > 0.5
        scores = lax.dot_general(queries, keys, nt, preferred_element_type=jnp.float32) * score_scale
        scores = jnp.where(keep, scores, MASKED)
        peak = jnp.max(scores, axis=1, keepdims=True)
        expanded = jnp.exp(scores - peak)
        probabilities = expanded / jnp.sum(expanded, axis=1, keepdims=True)
        rounded = probabilities.astype(jnp.bfloat16)
        att_ref[rows, :] = jnp.dot(rounded, values, preferred_element_type=jnp.float32).astype(att_ref.dtype)
        grad_probs = lax.dot_general(grads, values, nt, preferred_element_type=jnp.float32)
        centre = jnp.sum(grad_probs * probabilities, axis=1, keepdims=True)
        grad_scores = (probabilities * (grad_probs - centre) * score_scale).astype(jnp.bfloat16)
        gq_ref[rows, :] = jnp.dot(grad_scores, keys, preferred_element_type=jnp.float32).astype(gq_ref.dtype)
        grad_keys = grad_keys + lax.dot_general(grad_scores, queries, tn, preferred_element_type=jnp.float32)
        grad_values = grad_values + lax.dot_general(rounded, grads, tn, preferred_element_type=jnp.float32)
    for side, side_ref in enumerate((low_ref, own_ref, high_ref)):
        part = slice(side * block_rows, (side + 1) * block_rows)
        side_ref[0] = grad_keys[part].astype(side_ref.dtype)
        side_ref[1] = grad_values[part].astype(side_ref.dtype)


def fused_attention(keep_rows, queries, keyvals, low, high, grad_attended, heads):
    rows, width = grad_attended.shape
    head_dim = width // heads
    span = 3 * rows

    def column(offset):
        return pl.BlockSpec((rows, head_dim), lambda h: (0, h + offset))

    m_spec = pl.BlockSpec(keep_rows.shape, lambda h: (0, 0))
    cost = pl.CostEstimate(flops=12 * rows * span * width, transcendentals=rows * span * heads,
                           bytes_accessed=2 * (3 * rows * width + 2 * span * width) + 4 * (2 * rows * width) + 2 * (5 * rows * width))
    bf16_out = jax.ShapeDtypeStruct((rows, width), jnp.bfloat16)
    pair_spec = pl.BlockSpec((2, rows, head_dim), lambda h: (0, 0, h))
    return pl.pallas_call(
        attention_kernel,
        grid=(heads,),
        in_specs=[m_spec, column(0), column(0), column(heads), column(0), column(heads),
                  column(0), column(heads), column(0)],
        out_specs=[column(0), column(0), pair_spec, pair_spec, pair_spec],
        out_shape=[
            bf16_out,
            bf16_out,
            jax.ShapeDtypeStruct((2, rows, width), jnp.float32),
            jax.ShapeDtypeStruct((2, rows, width), jnp.bfloat16),
            jax.ShapeDtypeStruct((2, rows, width), jnp.bfloat16),
        ],
        cost_estimate=cost,
    )(keep_rows, queries, keyvals, keyvals, low, low, high, high, grad_attended)


def device_step(tokens, cotangent, w_qkv, w_out, norm_gain, tile_lists, tile_counts):
    own_tokens = tokens[0]
    own_grads = cotangent[0]
    row_count, model_width = own_tokens.shape
    tile_count = row_count // TILE
    tile_total = tile_lists.shape[0]
    device = lax.axis_index("node")
    own_lists = lax.dynamic_slice_in_dim(tile_lists, device * tile_count, tile_count, 0)
    own_counts = lax.dynamic_slice_in_dim(tile_counts, device * tile_count, tile_count, 0)
    allowed = tile_mask(own_lists, own_counts, (device - 1) * tile_count, tile_total)
    widened = own_tokens.astype(jnp.float32)
    inverse_rms = lax.rsqrt(jnp.mean(widened * widened, axis=-1, keepdims=True) + EPS)
    unit_rows = widened * inverse_rms
    normed = (unit_rows * norm_gain).astype(jnp.bfloat16)
    keyvals = jnp.dot(normed, w_qkv[:, model_width:], preferred_element_type=jnp.float32).astype(
        jnp.bfloat16
    )
    queries = jnp.dot(normed, w_qkv[:, :model_width], preferred_element_type=jnp.float32).astype(
        jnp.bfloat16
    )
    low = passed_along(keyvals, "node", 1)
    high = passed_along(keyvals, "node", -1)
    contract_rows = (((0,), (0,)), ((), ()))
    contract_cols = (((1,), (1,)), ((), ()))
    grad_attended = lax.dot_general(
        own_grads, w_out, contract_cols, preferred_element_type=jnp.float32
    ).astype(jnp.bfloat16)
    keep_rows = jnp.zeros((8, 3 * row_count), jnp.float32)
    keep_rows = keep_rows.at[:tile_count].set(jnp.repeat(allowed, TILE, axis=1).astype(jnp.float32))
    attended, grad_q, grad_own, grad_low, grad_high = fused_attention(
        keep_rows, queries, keyvals, low, high, grad_attended, HEADS
    )
    outputs = (widened + jnp.dot(attended, w_out, preferred_element_type=jnp.float32)).astype(
        jnp.bfloat16
    )
    term_out = lax.dot_general(
        attended, own_grads, contract_rows, preferred_element_type=jnp.float32
    )
    term_q = lax.dot_general(normed, grad_q, contract_rows, preferred_element_type=jnp.float32)
    early = chip_sum(jnp.concatenate([term_q, term_out], axis=1))
    grad_pair = grad_own
    for offset, side_part in ((-1, grad_low), (1, grad_high)):
        arrived = passed_along(side_part, "node", offset)
        grad_pair = grad_pair + arrived.astype(jnp.float32)
    grad_keyvals = jnp.concatenate([grad_pair[0], grad_pair[1]], axis=1)
    grad_kv = grad_keyvals.astype(jnp.bfloat16)
    term_kv = lax.dot_general(normed, grad_kv, contract_rows, preferred_element_type=jnp.float32)
    grad_normed = lax.dot_general(
        grad_q, w_qkv[:, :model_width], contract_cols, preferred_element_type=jnp.float32
    ) + lax.dot_general(
        grad_kv, w_qkv[:, model_width:], contract_cols, preferred_element_type=jnp.float32
    )
    term_gain = jnp.sum(grad_normed * unit_rows, axis=0)
    grad_unit = grad_normed * norm_gain
    inner_mean = jnp.mean(grad_unit * unit_rows, axis=-1, keepdims=True)
    grad_tokens = (
        own_grads.astype(jnp.float32) + inverse_rms * (grad_unit - unit_rows * inner_mean)
    ).astype(jnp.bfloat16)
    gain_block = jnp.zeros((model_width, 128), jnp.float32).at[:, 0].set(term_gain)
    late = chip_sum(jnp.concatenate([term_kv, gain_block], axis=1))
    return (outputs[None], grad_tokens[None]) + node_sum(early, late, model_width)


def section_order(rows):
    y_size, x_size, core_size = lax.axis_size("y"), lax.axis_size("x"), lax.axis_size("core")
    shape = rows.shape
    split = rows.reshape((y_size, x_size, core_size, -1) + shape[1:])
    return jnp.moveaxis(split, (2, 1, 0), (0, 1, 2)).reshape(shape)


def exchange_sum(block, axis):
    count = lax.axis_size(axis)
    pieces = block.reshape((count, block.shape[0] // count) + block.shape[1:])
    return wide_sum(lax.all_to_all(pieces.astype(jnp.bfloat16), axis, 0, 0, tiled=False))


def wide_sum(pieces):
    return jnp.sum(pieces.astype(jnp.float32), axis=0)


def node_sum(early, late, model_width):
    joined = jnp.concatenate([early, late], axis=1)
    for axis in ("x", "y"):
        joined = exchange_sum(joined, axis)
    early, late = joined[:, : 2 * model_width], joined[:, 2 * model_width :]
    node_count = lax.axis_size("node")
    own_rows = early.shape[0]
    qkv = jnp.concatenate([early[:, :model_width], late[:, : 2 * model_width]], axis=1)
    rest = jnp.concatenate([early[:, model_width:], late[:, 2 * model_width :]], axis=1)
    qkv_blocks = jnp.moveaxis(qkv.reshape(own_rows, node_count, -1), 1, 0)
    shared = jnp.broadcast_to(rest[None], (node_count,) + rest.shape)
    mixed = jnp.concatenate([qkv_blocks, shared], axis=2)
    summed = wide_sum(lax.all_to_all(mixed.astype(jnp.bfloat16), "node", 0, 0, tiled=False))
    block_width = qkv.shape[1] // node_count
    part_qkv = summed[:, :block_width]
    part_out = summed[:, block_width : block_width + model_width]
    part_gain = summed[:, block_width + model_width]
    return (part_qkv, part_out, part_gain)


def chip_sum(term):
    return exchange_sum(section_order(term), "core")


def solution(mesh):
    node_size, section_size = mesh.devices.shape
    core_size = 2
    x_size = 4
    y_size = section_size // (core_size * x_size)
    fine = Mesh(mesh.devices.reshape(node_size, y_size, x_size, core_size), ("node", "y", "x", "core"))
    section = ("y", "x", "core")
    return jax.shard_map(
        device_step,
        mesh=fine,
        in_specs=(P(section, "node", None), P(section, "node", None), P(), P(), P(), P(), P()),
        out_specs=(
            P(section, "node", None),
            P(section, "node", None),
            P(section, "node"),
            P(section, None),
            P(section),
        ),
        check_vma=False,
    )
```
